32 devices in a mesh: grp: 2 (over y), blk: 8 (over z, core), tm: 2 (over x), rep: 1.
Axes of the slice: x: 2, y: 2, z: 4, core: 2. Of those that a mesh axis runs over, the one named last changes fastest.
Arguments:
- factor_rows: bfloat16 [8192, 2048], P(('grp', 'blk')), parts along dimension 0, may hold values from -0.125 to 0.125
- noise: bfloat16 [8192, 8192], P(('grp', 'blk'), ('tm', 'rep')), parts along dimension 0, may hold values from -6 to 6
- time_kernel: float32 [8192], replicated, may hold values from -0.0625 to 0.0625
- region_of_block: int32 [16], P('grp'), parts along dimension 0, may hold values from 0 to 3, as said below
Outputs:
- field: bfloat16 [8192, 8192], P(('grp', 'blk', 'tm', 'rep')), parts along dimension 0
The draws below stay inside these ranges and needn't reach their ends.
There are 2 independent parts, one for each index of `grp`. The reference program is written for one: setup_inputs(seed, part) draws one part's arguments, and reference() takes and returns one part's arrays. A program takes and returns all parts, laid end to end along the dimension named above; an argument that names none is the same for every part. Nothing has to cross between parts.
Inputs may be any that keep to these rules, and one draw needn't show every extreme that they name: `region_of_block`: each part is its own table: within one part, the blocks of one region are consecutive, region numbers never fall from block to block and every region from 0 to 3 appears; a region holds 1 to 4 blocks, and some region holds exactly 4. The next part starts again at region 0.
All inputs are finite; a program needn't handle non-finite values.
Results may differ from the reference program's by a relative error of at most 0.0049.
Values may be sent and summed in bfloat16 or wider, within the bound.
No kernel may reach another device: no remote copies, remote signals or barrier semaphores. Data moves between devices by JAX's collectives and lax.ppermute only.
A program may use at most 128 MiB of HBM per device.

```python
import jax
import jax.numpy as jnp
from jax import lax

BLOCK = 512
MAXC = 4
DAYS = 8192
BLOCKS = 8
STATIONS = 4096
REGIONS = 4


def draw_region_of_block(key, part):
    order = jax.random.permutation(jax.random.fold_in(key, 7), REGIONS)
    rank = jnp.argsort(order).astype(jnp.int32)
    lengths = jnp.where(rank == 0, MAXC, jnp.where(rank <= MAXC - 2, 1, 2)).astype(jnp.int32)
    ends = jnp.cumsum(lengths).astype(jnp.int32)
    block_ids = jnp.arange(BLOCKS, dtype=jnp.int32)
    return jnp.sum((ends[None, :] <= block_ids[:, None]).astype(jnp.int32), axis=1).astype(jnp.int32)


def block_scale(own_key, extent, shards, least, top_value):
    def one(dim, parts):
        draws = jax.random.uniform(jax.random.fold_in(jax.random.fold_in(own_key, 6), dim), (parts,), jnp.float32, least / len(shards), top_value / len(shards))
        return jnp.repeat(jnp.exp(draws), extent[dim] // parts).reshape((-1,) + (1,) * (len(extent) - dim - 1))

    level = one(*shards[0])
    for cut in shards[1:]:
        level = level * one(*cut)
    return level


def scatter_about(stream_key, extent, deviation, reach, pieces=(), held_as=jnp.bfloat16):
    loudness = block_scale(stream_key, extent, pieces, -0.22, 0.18) if pieces else 1.0
    values = jax.random.normal(stream_key, extent, jnp.float32) * deviation * loudness
    return jnp.minimum(jnp.maximum(values, -reach), reach).astype(held_as)


def setup_inputs(seed: int = 0, part: int = 0) -> dict:
    keys = jax.random.split(jax.random.key(seed), 5)
    own_keys = jax.random.split(jax.random.fold_in(keys[4], part), 5)
    return {
        "factor_rows": scatter_about(own_keys[0], (STATIONS, MAXC * BLOCK), (MAXC * BLOCK) ** -0.5, 0.125, ((0, 8),)),
        "noise": scatter_about(own_keys[1], (STATIONS, DAYS), 1.0, 6.0, ((0, 8), (1, 2))),
        "time_kernel": scatter_about(keys[2], (DAYS,), DAYS ** -0.5, 0.0625, (), jnp.float32),
        "region_of_block": draw_region_of_block(jax.random.fold_in(jax.random.fold_in(keys[4], part), 71), part),
    }


def reference(factor_rows, noise, time_kernel, region_of_block):
    blocks = noise.shape[0] // BLOCK
    row_ids = lax.broadcasted_iota(jnp.int32, (BLOCK, BLOCK), 0)
    col_ids = lax.broadcasted_iota(jnp.int32, (BLOCK, BLOCK), 1)
    lower = row_ids >= col_ids
    kernel_spectrum = jnp.fft.rfft(time_kernel.astype(jnp.float32))

    def one_block(index):
        rows = lax.dynamic_slice_in_dim(factor_rows, (index * BLOCK).astype(jnp.int32), BLOCK, 0).astype(jnp.float32)
        own = region_of_block[index]
        total = jnp.zeros((BLOCK, DAYS), jnp.float32)
        for step in range(MAXC):
            source = jnp.maximum(index - step, 0).astype(jnp.int32)
            valid = (index >= step) & (region_of_block[source] == own)
            tile = rows[:, step * BLOCK:(step + 1) * BLOCK]
            if step == 0:
                tile = jnp.where(lower, tile, jnp.zeros_like(tile))
            part = lax.dynamic_slice_in_dim(noise, (source * BLOCK).astype(jnp.int32), BLOCK, 0).astype(jnp.float32)
            product = jnp.dot(tile, part, preferred_element_type=jnp.float32, precision=lax.Precision.HIGHEST)
            total = total + jnp.where(valid, product, jnp.zeros_like(product))
        spatial = lax.optimization_barrier(total.astype(jnp.bfloat16)).astype(jnp.float32)
        filtered = jnp.fft.irfft(jnp.fft.rfft(spatial, axis=1) * kernel_spectrum[None, :], n=DAYS, axis=1)
        return filtered.astype(jnp.bfloat16)

    result = lax.map(one_block, jnp.arange(blocks, dtype=jnp.int32))
    return result.reshape(blocks * BLOCK, DAYS)
```

```python
import math

import jax
import jax.numpy as jnp
from jax import lax
from jax.sharding import PartitionSpec as P

FIRST = 64
CHUNKS = 4


def shifted(block, axis, distance):
    devices = range(lax.axis_size(axis))
    route = [(i - distance, i) for i in devices if i - distance in devices]
    return lax.ppermute(block, axis, route)


def make_tables(first, second):
    total = first * second
    row_a = lax.broadcasted_iota(jnp.int32, (first, first), 0)
    col_a = lax.broadcasted_iota(jnp.int32, (first, first), 1)
    angle_one = 2.0 * math.pi / first * (row_a * col_a % first).astype(jnp.float32)
    row_t = lax.broadcasted_iota(jnp.int32, (first, second), 0)
    col_t = lax.broadcasted_iota(jnp.int32, (first, second), 1)
    angle_tw = 2.0 * math.pi / total * (row_t * col_t % total).astype(jnp.float32)
    row_b = lax.broadcasted_iota(jnp.int32, (second, second), 0)
    col_b = lax.broadcasted_iota(jnp.int32, (second, second), 1)
    angle_two = 2.0 * math.pi / second * (row_b * col_b % second).astype(jnp.float32)
    return (
        jnp.cos(angle_one),
        -jnp.sin(angle_one),
        jnp.cos(angle_tw),
        -jnp.sin(angle_tw),
        jnp.cos(angle_two),
        -jnp.sin(angle_two),
    )


def left_apply(table, values):
    return jnp.einsum(
        "kn,rnm->rkm", table, values.astype(jnp.float32), precision=lax.Precision.HIGH
    )


def right_apply(values, table):
    return jnp.einsum("rkn,nm->rkm", values, table, precision=lax.Precision.HIGH)


def forward(sig_re, sig_im, tables):
    one_re, one_im, tw_re, tw_im, two_re, two_im = tables
    first_re = left_apply(one_re, sig_re) - left_apply(one_im, sig_im)
    first_im = left_apply(one_re, sig_im) + left_apply(one_im, sig_re)
    turned_re = first_re * tw_re - first_im * tw_im
    turned_im = first_re * tw_im + first_im * tw_re
    spec_re = right_apply(turned_re, two_re) - right_apply(turned_im, two_im)
    spec_im = right_apply(turned_re, two_im) + right_apply(turned_im, two_re)
    return (spec_re, spec_im)


def inverse(spec_re, spec_im, tables):
    one_re, one_im, tw_re, tw_im, two_re, two_im = tables
    back_re = right_apply(spec_re, two_re) + right_apply(spec_im, two_im)
    back_im = right_apply(spec_im, two_re) - right_apply(spec_re, two_im)
    turned_re = back_re * tw_re + back_im * tw_im
    turned_im = back_im * tw_re - back_re * tw_im
    total = one_re.shape[0] * two_re.shape[0]
    out_re = (left_apply(one_re, turned_re) + left_apply(one_im, turned_im)) / total
    out_im = (left_apply(one_re, turned_im) - left_apply(one_im, turned_re)) / total
    return (out_re, out_im)


def on_device(factor_rows, noise, time_kernel, region_of_block):
    width = noise.shape[0]
    slots = factor_rows.shape[1] // width
    position = lax.axis_index("blk")
    own_region = lax.dynamic_index_in_dim(region_of_block, position, 0, keepdims=False)
    row_ids = lax.broadcasted_iota(jnp.int32, (width, width), 0)
    col_ids = lax.broadcasted_iota(jnp.int32, (width, width), 1)
    tiles = [
        jnp.where(
            row_ids >= col_ids, factor_rows[:, :width], jnp.zeros((width, width), jnp.bfloat16)
        )
    ]
    valid = [None]
    for step in range(1, slots):
        tiles.append(factor_rows[:, step * width : (step + 1) * width])
        source = jnp.maximum(position - step, 0)
        source_region = lax.dynamic_index_in_dim(region_of_block, source, 0, keepdims=False)
        valid.append((position >= step) & (source_region == own_region))
    pieces = []
    for piece in jnp.split(noise, CHUNKS, axis=1):
        total = jnp.dot(tiles[0], piece, preferred_element_type=jnp.float32)
        carried = piece
        for step in range(1, slots):
            carried = shifted(carried, "blk", 1)
            product = jnp.dot(tiles[step], carried, preferred_element_type=jnp.float32)
            total = total + jnp.where(valid[step], product, jnp.zeros_like(product))
        pieces.append(total.astype(jnp.bfloat16))
    spatial = jnp.concatenate(pieces, axis=1)
    regrouped = lax.all_to_all(spatial, ("tm", "rep"), split_axis=0, concat_axis=1, tiled=True)
    days = regrouped.shape[1]
    stations = regrouped.shape[0]
    second = days // FIRST
    tables = make_tables(FIRST, second)
    paired = regrouped.reshape(stations // 2, 2, FIRST, second)
    sig_re = paired[:, 0]
    sig_im = paired[:, 1]
    kernel_sig = time_kernel.reshape(1, FIRST, second)
    kernel_re, kernel_im = forward(kernel_sig, jnp.zeros_like(kernel_sig), tables)
    spec_re, spec_im = forward(sig_re, sig_im, tables)
    prod_re = spec_re * kernel_re - spec_im * kernel_im
    prod_im = spec_re * kernel_im + spec_im * kernel_re
    out_re, out_im = inverse(prod_re, prod_im, tables)
    joined = jnp.stack((out_re, out_im), axis=1)
    return joined.reshape(stations, days).astype(jnp.bfloat16)


def solution(mesh):
    placed = (P(("grp", "blk"), None), P(("grp", "blk"), ("tm", "rep")), P(), P("grp"))
    return jax.shard_map(
        on_device,
        mesh=mesh,
        in_specs=placed,
        out_specs=P(("grp", "blk", "tm", "rep"), None),
        check_vma=False,
    )
```

```python
import math

import jax
import jax.numpy as jnp
from jax import lax
from jax.sharding import PartitionSpec as P

FIRST = 64
CHUNKS = 4


def shifted(block, axis, distance):
    devices = range(lax.axis_size(axis))
    route = [(i - distance, i) for i in devices if i - distance in devices]
    return lax.ppermute(block, axis, route)


def make_tables(first, second):
    total = first * second
    row_a = lax.broadcasted_iota(jnp.int32, (first, first), 0)
    col_a = lax.broadcasted_iota(jnp.int32, (first, first), 1)
    angle_one = 2.0 * math.pi / first * (row_a * col_a % first).astype(jnp.float32)
    row_t = lax.broadcasted_iota(jnp.int32, (first, second), 0)
    col_t = lax.broadcasted_iota(jnp.int32, (first, second), 1)
    angle_tw = 2.0 * math.pi / total * (row_t * col_t % total).astype(jnp.float32)
    row_b = lax.broadcasted_iota(jnp.int32, (second, second), 0)
    col_b = lax.broadcasted_iota(jnp.int32, (second, second), 1)
    angle_two = 2.0 * math.pi / second * (row_b * col_b % second).astype(jnp.float32)
    return (
        jnp.cos(angle_one),
        -jnp.sin(angle_one),
        jnp.cos(angle_tw),
        -jnp.sin(angle_tw),
        jnp.cos(angle_two),
        -jnp.sin(angle_two),
    )


def left_apply(table, values):
    return jnp.einsum(
        "kn,rnm->rkm", table, values.astype(jnp.float32), precision=lax.Precision.HIGH
    )


def right_apply(values, table):
    return jnp.einsum("rkn,nm->rkm", values, table, precision=lax.Precision.HIGH)


def forward(sig_re, sig_im, tables):
    one_re, one_im, tw_re, tw_im, two_re, two_im = tables
    first_re = left_apply(one_re, sig_re) - left_apply(one_im, sig_im)
    first_im = left_apply(one_re, sig_im) + left_apply(one_im, sig_re)
    turned_re = first_re * tw_re - first_im * tw_im
    turned_im = first_re * tw_im + first_im * tw_re
    spec_re = right_apply(turned_re, two_re) - right_apply(turned_im, two_im)
    spec_im = right_apply(turned_re, two_im) + right_apply(turned_im, two_re)
    return (spec_re, spec_im)


def inverse(spec_re, spec_im, tables):
    one_re, one_im, tw_re, tw_im, two_re, two_im = tables
    back_re = right_apply(spec_re, two_re) + right_apply(spec_im, two_im)
    back_im = right_apply(spec_im, two_re) - right_apply(spec_re, two_im)
    turned_re = back_re * tw_re + back_im * tw_im
    turned_im = back_im * tw_re - back_re * tw_im
    total = one_re.shape[0] * two_re.shape[0]
    out_re = (left_apply(one_re, turned_re) + left_apply(one_im, turned_im)) / total
    out_im = (left_apply(one_re, turned_im) - left_apply(one_im, turned_re)) / total
    return (out_re, out_im)


def on_device(factor_rows, noise, time_kernel, region_of_block):
    width = noise.shape[0]
    slots = factor_rows.shape[1] // width
    position = lax.axis_index("blk")
    own_region = lax.dynamic_index_in_dim(region_of_block, position, 0, keepdims=False)
    row_ids = lax.broadcasted_iota(jnp.int32, (width, width), 0)
    col_ids = lax.broadcasted_iota(jnp.int32, (width, width), 1)
    tiles = [
        jnp.where(
            row_ids >= col_ids, factor_rows[:, :width], jnp.zeros((width, width), jnp.bfloat16)
        )
    ]
    valid = [None]
    for step in range(1, slots):
        tiles.append(factor_rows[:, step * width : (step + 1) * width])
        source = jnp.maximum(position - step, 0)
        source_region = lax.dynamic_index_in_dim(region_of_block, source, 0, keepdims=False)
        valid.append((position >= step) & (source_region == own_region))
    pieces = []
    for piece in jnp.split(noise, CHUNKS, axis=1):
        total = jnp.dot(tiles[0], piece, preferred_element_type=jnp.float32)
        carried = piece
        for step in range(1, slots):
            carried = shifted(carried, "blk", 1)
            product = jnp.dot(tiles[step], carried, preferred_element_type=jnp.float32)
            total = total + jnp.where(valid[step], product, jnp.zeros_like(product))
        spatial = total.astype(jnp.bfloat16)
        pieces.append(
            lax.all_to_all(spatial, ("tm", "rep"), split_axis=0, concat_axis=1, tiled=True)
        )
    sources = lax.axis_size(("tm", "rep"))
    stations = pieces[0].shape[0]
    chunk = noise.shape[1] // CHUNKS
    stacked = jnp.stack(
        [piece.reshape(stations, sources, chunk) for piece in pieces], axis=2
    )
    regrouped = stacked.reshape(stations, sources * CHUNKS * chunk)
    days = regrouped.shape[1]
    stations = regrouped.shape[0]
    second = days // FIRST
    tables = make_tables(FIRST, second)
    paired = regrouped.reshape(stations // 2, 2, FIRST, second)
    sig_re = paired[:, 0]
    sig_im = paired[:, 1]
    kernel_sig = time_kernel.reshape(1, FIRST, second)
    kernel_re, kernel_im = forward(kernel_sig, jnp.zeros_like(kernel_sig), tables)
    spec_re, spec_im = forward(sig_re, sig_im, tables)
    prod_re = spec_re * kernel_re - spec_im * kernel_im
    prod_im = spec_re * kernel_im + spec_im * kernel_re
    out_re, out_im = inverse(prod_re, prod_im, tables)
    joined = jnp.stack((out_re, out_im), axis=1)
    return joined.reshape(stations, days).astype(jnp.bfloat16)


def solution(mesh):
    placed = (P(("grp", "blk"), None), P(("grp", "blk"), ("tm", "rep")), P(), P("grp"))
    return jax.shard_map(
        on_device,
        mesh=mesh,
        in_specs=placed,
        out_specs=P(("grp", "blk", "tm", "rep"), None),
        check_vma=False,
    )
```

```python
import math

import jax
import jax.numpy as jnp
from jax import lax
from jax.sharding import PartitionSpec as P

FIRST = 64
CHUNKS = 4


def shifted(block, axis, distance):
    devices = range(lax.axis_size(axis))
    route = [(i - distance, i) for i in devices if i - distance in devices]
    return lax.ppermute(block, axis, route)


def filter_days(x, time_kernel, first):
    stations, days = x.shape
    second = days // first
    half = first // 2 + 1
    k = lax.broadcasted_iota(jnp.int32, (half, first), 0)
    a = lax.broadcasted_iota(jnp.int32, (half, first), 1)
    angle = 2.0 * math.pi / first * (k * a % first).astype(jnp.float32)
    forward = jnp.stack((jnp.cos(angle), -jnp.sin(angle)), axis=1)
    spectrum = jnp.einsum(
        "kra,ab->krb", forward, time_kernel.reshape(first, second),
        precision=lax.Precision.HIGHEST,
    )
    d = lax.broadcasted_iota(jnp.int32, (second, second), 0)
    c = lax.broadcasted_iota(jnp.int32, (second, second), 1)
    lag = (d - c) % second
    base_re = spectrum[:, 0][:, lag]
    base_im = spectrum[:, 1][:, lag]
    turn = 2.0 * math.pi / first * jnp.arange(half, dtype=jnp.float32)
    cos_k = jnp.cos(turn)[:, None, None]
    sin_k = jnp.sin(turn)[:, None, None]
    wrapped = (d < c)[None]
    mat_re = jnp.where(wrapped, base_re * cos_k + base_im * sin_k, base_re)
    mat_im = jnp.where(wrapped, base_im * cos_k - base_re * sin_k, base_im)
    mat_re_t = jnp.swapaxes(mat_re, 1, 2)
    mat_im_t = jnp.swapaxes(mat_im, 1, 2)
    blocks = jnp.concatenate(
        (
            jnp.concatenate((mat_re_t, mat_im_t), axis=2),
            jnp.concatenate((-mat_im_t, mat_re_t), axis=2),
        ),
        axis=1,
    )
    weight = jnp.where((k[:, 0] == 0) | (k[:, 0] == first // 2), 1.0, 2.0) / first
    inverse = jnp.stack(
        (jnp.cos(angle) * weight[:, None], -jnp.sin(angle) * weight[:, None]), axis=1
    )
    forward_hi = forward.astype(jnp.bfloat16)
    forward_lo = (forward - forward_hi.astype(jnp.float32)).astype(jnp.bfloat16)
    grid = x.reshape(stations, first, second)
    lifted = jnp.einsum(
        "kra,sab->ksrb", forward_hi, grid, preferred_element_type=jnp.float32
    ) + jnp.einsum("kra,sab->ksrb", forward_lo, grid, preferred_element_type=jnp.float32)
    mixed = jnp.einsum(
        "ksi,kij->ksj", lifted.reshape(half, stations, 2 * second), blocks,
        precision=lax.Precision.HIGH, preferred_element_type=jnp.float32,
    )
    out = jnp.einsum(
        "kra,ksrb->sab", inverse, mixed.reshape(half, stations, 2, second),
        precision=lax.Precision.HIGH, preferred_element_type=jnp.float32,
    )
    return out.reshape(stations, days).astype(jnp.bfloat16)


def on_device(factor_rows, noise, time_kernel, region_of_block):
    width = noise.shape[0]
    slots = factor_rows.shape[1] // width
    position = lax.axis_index("blk")
    own_region = lax.dynamic_index_in_dim(region_of_block, position, 0, keepdims=False)
    row_ids = lax.broadcasted_iota(jnp.int32, (width, width), 0)
    col_ids = lax.broadcasted_iota(jnp.int32, (width, width), 1)
    tiles = [
        jnp.where(
            row_ids >= col_ids, factor_rows[:, :width], jnp.zeros((width, width), jnp.bfloat16)
        )
    ]
    valid = [None]
    for step in range(1, slots):
        tiles.append(factor_rows[:, step * width : (step + 1) * width])
        source = jnp.maximum(position - step, 0)
        source_region = lax.dynamic_index_in_dim(region_of_block, source, 0, keepdims=False)
        valid.append((position >= step) & (source_region == own_region))
    pieces = []
    for piece in jnp.split(noise, CHUNKS, axis=1):
        total = jnp.dot(tiles[0], piece, preferred_element_type=jnp.float32)
        carried = piece
        for step in range(1, slots):
            carried = shifted(carried, "blk", 1)
            product = jnp.dot(tiles[step], carried, preferred_element_type=jnp.float32)
            total = total + jnp.where(valid[step], product, jnp.zeros_like(product))
        spatial = total.astype(jnp.bfloat16)
        pieces.append(
            lax.all_to_all(spatial, ("tm", "rep"), split_axis=0, concat_axis=1, tiled=True)
        )
    sources = lax.axis_size(("tm", "rep"))
    stations = pieces[0].shape[0]
    chunk = noise.shape[1] // CHUNKS
    stacked = jnp.stack(
        [piece.reshape(stations, sources, chunk) for piece in pieces], axis=2
    )
    regrouped = stacked.reshape(stations, sources * CHUNKS * chunk)
    return filter_days(regrouped, time_kernel, FIRST)


def solution(mesh):
    placed = (P(("grp", "blk"), None), P(("grp", "blk"), ("tm", "rep")), P(), P("grp"))
    return jax.shard_map(
        on_device,
        mesh=mesh,
        in_specs=placed,
        out_specs=P(("grp", "blk", "tm", "rep"), None),
        check_vma=False,
    )
```

```python
import math

import jax
import jax.numpy as jnp
from jax import lax
from jax.sharding import PartitionSpec as P

FIRST = 64
CHUNKS = 4


def shifted(block, axis, distance):
    devices = range(lax.axis_size(axis))
    route = [(i - distance, i) for i in devices if i - distance in devices]
    return lax.ppermute(block, axis, route)


def filter_days(grid, time_kernel):
    first, stations, second = grid.shape
    half = first // 2 + 1
    k = lax.broadcasted_iota(jnp.int32, (half, first), 0)
    a = lax.broadcasted_iota(jnp.int32, (half, first), 1)
    angle = 2.0 * math.pi / first * (k * a % first).astype(jnp.float32)
    cos_t = jnp.cos(angle)
    sin_t = jnp.sin(angle)
    taps = time_kernel.reshape(first, second)
    spec_re = jnp.dot(cos_t, taps, precision=lax.Precision.HIGHEST)
    spec_im = -jnp.dot(sin_t, taps, precision=lax.Precision.HIGHEST)
    turn = 2.0 * math.pi / first * jnp.arange(half, dtype=jnp.float32)
    cos_k = jnp.cos(turn)[:, None]
    sin_k = jnp.sin(turn)[:, None]
    ext_re = jnp.concatenate((spec_re, spec_re * cos_k + spec_im * sin_k), axis=1)
    ext_im = jnp.concatenate((spec_im, spec_im * cos_k - spec_re * sin_k), axis=1)

    def toeplitz(ext):
        tiled = jnp.tile(ext, (1, second))[:, : second * (2 * second - 1)]
        return tiled.reshape(half, second, 2 * second - 1)[:, :, :second]

    mat_re = toeplitz(ext_re)
    mat_im = toeplitz(ext_im)
    forward = jnp.concatenate((cos_t, -sin_t), axis=0)
    forward_hi = forward.astype(jnp.bfloat16)
    forward_lo = (forward - forward_hi.astype(jnp.float32)).astype(jnp.bfloat16)
    flat = grid.reshape(first, stations * second)
    lifted = jnp.dot(forward_hi, flat, preferred_element_type=jnp.float32) + jnp.dot(
        forward_lo, flat, preferred_element_type=jnp.float32
    )
    x_re = lifted[:half].reshape(half, stations, second)
    x_im = lifted[half:].reshape(half, stations, second)

    def mix(u, m):
        return jnp.einsum(
            "ksc,kcd->ksd", u, m,
            precision=lax.Precision.HIGH, preferred_element_type=jnp.float32,
        )

    y_re = mix(x_re, mat_re) - mix(x_im, mat_im)
    y_im = mix(x_re, mat_im) + mix(x_im, mat_re)
    weight = jnp.where((k[:, :1] == 0) | (k[:, :1] == first // 2), 1.0, 2.0) / first
    inv_re = jnp.transpose(cos_t * weight)
    inv_im = jnp.transpose(-sin_t * weight)
    out = jnp.dot(
        inv_re, y_re.reshape(half, stations * second), precision=lax.Precision.HIGH
    ) + jnp.dot(inv_im, y_im.reshape(half, stations * second), precision=lax.Precision.HIGH)
    out = out.astype(jnp.bfloat16).reshape(first, stations, second)
    return jnp.transpose(out, (1, 0, 2)).reshape(stations, first * second)


def on_device(factor_rows, noise, time_kernel, region_of_block):
    width = noise.shape[0]
    slots = factor_rows.shape[1] // width
    position = lax.axis_index("blk")
    own_region = lax.dynamic_index_in_dim(region_of_block, position, 0, keepdims=False)
    row_ids = lax.broadcasted_iota(jnp.int32, (width, width), 0)
    col_ids = lax.broadcasted_iota(jnp.int32, (width, width), 1)
    tiles = [
        jnp.where(
            row_ids >= col_ids, factor_rows[:, :width], jnp.zeros((width, width), jnp.bfloat16)
        )
    ]
    valid = [None]
    for step in range(1, slots):
        tiles.append(factor_rows[:, step * width : (step + 1) * width])
        source = jnp.maximum(position - step, 0)
        source_region = lax.dynamic_index_in_dim(region_of_block, source, 0, keepdims=False)
        valid.append((position >= step) & (source_region == own_region))
    pieces = []
    for piece in jnp.split(noise, CHUNKS, axis=1):
        total = jnp.dot(tiles[0], piece, preferred_element_type=jnp.float32)
        carried = piece
        for step in range(1, slots):
            carried = shifted(carried, "blk", 1)
            product = jnp.dot(tiles[step], carried, preferred_element_type=jnp.float32)
            total = total + jnp.where(valid[step], product, jnp.zeros_like(product))
        spatial = total.astype(jnp.bfloat16)
        pieces.append(
            lax.all_to_all(spatial, ("tm", "rep"), split_axis=0, concat_axis=1, tiled=True)
        )
    sources = lax.axis_size(("tm", "rep"))
    stations = pieces[0].shape[0]
    days = time_kernel.shape[0]
    second = days // FIRST
    rows = noise.shape[1] // CHUNKS // second
    grid = jnp.stack(
        [
            jnp.transpose(piece.reshape(stations, sources, rows, second), (1, 2, 0, 3))
            for piece in pieces
        ],
        axis=1,
    )
    return filter_days(grid.reshape(FIRST, stations, second), time_kernel)


def solution(mesh):
    placed = (P(("grp", "blk"), None), P(("grp", "blk"), ("tm", "rep")), P(), P("grp"))
    return jax.shard_map(
        on_device,
        mesh=mesh,
        in_specs=placed,
        out_specs=P(("grp", "blk", "tm", "rep"), None),
        check_vma=False,
    )
```

```python
import math

import jax
import jax.numpy as jnp
from jax import lax
from jax.sharding import PartitionSpec as P

FIRST = 64
CHUNKS = 4


def shifted(block, axis, distance):
    devices = range(lax.axis_size(axis))
    route = [(i - distance, i) for i in devices if i - distance in devices]
    return lax.ppermute(block, axis, route)


def filter_tables(time_kernel, first):
    second = time_kernel.shape[0] // first
    half = first // 2 + 1
    k = lax.broadcasted_iota(jnp.int32, (half, first), 0)
    a = lax.broadcasted_iota(jnp.int32, (half, first), 1)
    angle = 2.0 * math.pi / first * (k * a % first).astype(jnp.float32)
    cos_t = jnp.cos(angle)
    sin_t = jnp.sin(angle)
    taps = time_kernel.reshape(first, second)
    spec_re = jnp.dot(cos_t, taps, precision=lax.Precision.HIGHEST)
    spec_im = -jnp.dot(sin_t, taps, precision=lax.Precision.HIGHEST)
    turn = 2.0 * math.pi / first * jnp.arange(half, dtype=jnp.float32)
    cos_k = jnp.cos(turn)[:, None]
    sin_k = jnp.sin(turn)[:, None]
    ext_re = jnp.concatenate((spec_re, spec_re * cos_k + spec_im * sin_k), axis=1)
    ext_im = jnp.concatenate((spec_im, spec_im * cos_k - spec_re * sin_k), axis=1)

    def toeplitz(ext):
        tiled = jnp.tile(ext, (1, second))[:, : second * (2 * second - 1)]
        return tiled.reshape(half, second, 2 * second - 1)[:, :, :second]

    forward = jnp.concatenate((cos_t, -sin_t), axis=0)
    forward_hi = forward.astype(jnp.bfloat16)
    forward_lo = (forward - forward_hi.astype(jnp.float32)).astype(jnp.bfloat16)
    weight = jnp.where((k[:, :1] == 0) | (k[:, :1] == first // 2), 1.0, 2.0) / first
    inv_re = jnp.transpose(cos_t * weight)
    inv_im = jnp.transpose(-sin_t * weight)
    return (toeplitz(ext_re), toeplitz(ext_im), forward_hi, forward_lo, inv_re, inv_im)


def lift(tables, piece, sources, chunks, index):
    forward_hi, forward_lo = tables[2], tables[3]
    width, first = forward_hi.shape
    stations = piece.shape[0]
    second = piece.shape[1] // sources // (first // sources // chunks)
    rows = first // sources // chunks
    block = jnp.transpose(piece.reshape(stations, sources, rows, second), (1, 2, 0, 3))
    block = block.reshape(sources * rows, stations * second)

    def part(table):
        return table.reshape(width, sources, chunks, rows)[:, :, index, :].reshape(width, -1)

    return jnp.dot(part(forward_hi), block, preferred_element_type=jnp.float32) + jnp.dot(
        part(forward_lo), block, preferred_element_type=jnp.float32
    )


def filter_rest(tables, lifted, stations):
    mat_re, mat_im, _, _, inv_re, inv_im = tables
    half, second = mat_re.shape[0], mat_re.shape[1]
    first = inv_re.shape[0]
    x_re = lifted[:half].reshape(half, stations, second)
    x_im = lifted[half:].reshape(half, stations, second)

    def mix(u, m):
        return jnp.einsum(
            "ksc,kcd->ksd", u, m,
            precision=lax.Precision.HIGH, preferred_element_type=jnp.float32,
        )

    y_re = mix(x_re, mat_re) - mix(x_im, mat_im)
    y_im = mix(x_re, mat_im) + mix(x_im, mat_re)
    out = jnp.dot(
        inv_re, y_re.reshape(half, stations * second), precision=lax.Precision.HIGH
    ) + jnp.dot(inv_im, y_im.reshape(half, stations * second), precision=lax.Precision.HIGH)
    out = out.astype(jnp.bfloat16).reshape(first, stations, second)
    return jnp.transpose(out, (1, 0, 2)).reshape(stations, first * second)


def on_device(factor_rows, noise, time_kernel, region_of_block):
    width = noise.shape[0]
    slots = factor_rows.shape[1] // width
    position = lax.axis_index("blk")
    own_region = lax.dynamic_index_in_dim(region_of_block, position, 0, keepdims=False)
    row_ids = lax.broadcasted_iota(jnp.int32, (width, width), 0)
    col_ids = lax.broadcasted_iota(jnp.int32, (width, width), 1)
    tiles = [
        jnp.where(
            row_ids >= col_ids, factor_rows[:, :width], jnp.zeros((width, width), jnp.bfloat16)
        )
    ]
    valid = [None]
    for step in range(1, slots):
        tiles.append(factor_rows[:, step * width : (step + 1) * width])
        source = jnp.maximum(position - step, 0)
        source_region = lax.dynamic_index_in_dim(region_of_block, source, 0, keepdims=False)
        valid.append((position >= step) & (source_region == own_region))
    tables = filter_tables(time_kernel, FIRST)
    sources = lax.axis_size(("tm", "rep"))
    lifted = None
    for index, piece in enumerate(jnp.split(noise, CHUNKS, axis=1)):
        total = jnp.dot(tiles[0], piece, preferred_element_type=jnp.float32)
        carried = piece
        for step in range(1, slots):
            carried = shifted(carried, "blk", 1)
            if index == 0 and step == 1:
                tables, carried = lax.optimization_barrier((tables, carried))
            product = jnp.dot(tiles[step], carried, preferred_element_type=jnp.float32)
            total = total + jnp.where(valid[step], product, jnp.zeros_like(product))
        spatial = total.astype(jnp.bfloat16)
        regrouped = lax.all_to_all(spatial, ("tm", "rep"), split_axis=0, concat_axis=1, tiled=True)
        part = lift(tables, regrouped, sources, CHUNKS, index)
        lifted = part if lifted is None else lifted + part
    return filter_rest(tables, lifted, regrouped.shape[0])


def solution(mesh):
    placed = (P(("grp", "blk"), None), P(("grp", "blk"), ("tm", "rep")), P(), P("grp"))
    return jax.shard_map(
        on_device,
        mesh=mesh,
        in_specs=placed,
        out_specs=P(("grp", "blk", "tm", "rep"), None),
        check_vma=False,
    )
```

```python
import math

import jax
import jax.numpy as jnp
from jax import lax
from jax.sharding import PartitionSpec as P

FIRST = 64
CHUNKS = 4


def shifted(block, axis, distance):
    devices = range(lax.axis_size(axis))
    route = [(i - distance, i) for i in devices if i - distance in devices]
    return lax.ppermute(block, axis, route)


def filter_tables(time_kernel, first):
    second = time_kernel.shape[0] // first
    half = first // 2 + 1
    k = lax.broadcasted_iota(jnp.int32, (half, first), 0)
    a = lax.broadcasted_iota(jnp.int32, (half, first), 1)
    angle = 2.0 * math.pi / first * (k * a % first).astype(jnp.float32)
    cos_t = jnp.cos(angle)
    sin_t = jnp.sin(angle)
    taps = time_kernel.reshape(first, second)
    spec_re = jnp.dot(cos_t, taps, precision=lax.Precision.HIGHEST)
    spec_im = -jnp.dot(sin_t, taps, precision=lax.Precision.HIGHEST)
    turn = 2.0 * math.pi / first * jnp.arange(half, dtype=jnp.float32)
    cos_k = jnp.cos(turn)[:, None]
    sin_k = jnp.sin(turn)[:, None]
    ext_re = jnp.concatenate((spec_re, spec_re * cos_k + spec_im * sin_k), axis=1)
    ext_im = jnp.concatenate((spec_im, spec_im * cos_k - spec_re * sin_k), axis=1)

    ext = jnp.concatenate((ext_re, ext_im), axis=0)
    ext_hi = ext.astype(jnp.bfloat16)
    ext_lo = (ext - ext_hi.astype(jnp.float32)).astype(jnp.bfloat16)
    lag = lax.broadcasted_iota(jnp.int32, (2 * second, second, second), 0)
    row = lax.broadcasted_iota(jnp.int32, (2 * second, second, second), 1)
    col = lax.broadcasted_iota(jnp.int32, (2 * second, second, second), 2)
    pick = (lag == (col - row) % (2 * second)).astype(jnp.bfloat16)
    both = jnp.dot(
        jnp.concatenate((ext_hi, ext_lo), axis=0),
        pick.reshape(2 * second, second * second),
        preferred_element_type=jnp.float32,
    )
    mats = (both[: 2 * half] + both[2 * half :]).reshape(2 * half, second, second)

    forward = jnp.concatenate((cos_t, -sin_t), axis=0)
    forward_hi = forward.astype(jnp.bfloat16)
    forward_lo = (forward - forward_hi.astype(jnp.float32)).astype(jnp.bfloat16)
    weight = jnp.where((k[:, :1] == 0) | (k[:, :1] == first // 2), 1.0, 2.0) / first
    inv_re = jnp.transpose(cos_t * weight)
    inv_im = jnp.transpose(-sin_t * weight)
    return (mats[:half], mats[half:], forward_hi, forward_lo, inv_re, inv_im)


def lift(tables, piece, sources, chunks, index):
    forward_hi, forward_lo = tables[2], tables[3]
    width, first = forward_hi.shape
    stations = piece.shape[0]
    second = piece.shape[1] // sources // (first // sources // chunks)
    rows = first // sources // chunks
    block = jnp.transpose(piece.reshape(stations, sources, rows, second), (1, 2, 0, 3))
    block = block.reshape(sources * rows, stations * second)

    def part(table):
        return table.reshape(width, sources, chunks, rows)[:, :, index, :].reshape(width, -1)

    return jnp.dot(part(forward_hi), block, preferred_element_type=jnp.float32) + jnp.dot(
        part(forward_lo), block, preferred_element_type=jnp.float32
    )


def filter_rest(tables, lifted, stations):
    mat_re, mat_im, _, _, inv_re, inv_im = tables
    half, second = mat_re.shape[0], mat_re.shape[1]
    first = inv_re.shape[0]
    x_re = lifted[:half].reshape(half, stations, second)
    x_im = lifted[half:].reshape(half, stations, second)

    def mix(u, m):
        return jnp.einsum(
            "ksc,kcd->ksd", u, m,
            precision=lax.Precision.HIGH, preferred_element_type=jnp.float32,
        )

    y_re = mix(x_re, mat_re) - mix(x_im, mat_im)
    y_im = mix(x_re, mat_im) + mix(x_im, mat_re)
    out = jnp.dot(
        inv_re, y_re.reshape(half, stations * second), precision=lax.Precision.HIGH
    ) + jnp.dot(inv_im, y_im.reshape(half, stations * second), precision=lax.Precision.HIGH)
    out = out.astype(jnp.bfloat16).reshape(first, stations, second)
    return jnp.transpose(out, (1, 0, 2)).reshape(stations, first * second)


def on_device(factor_rows, noise, time_kernel, region_of_block):
    width = noise.shape[0]
    slots = factor_rows.shape[1] // width
    position = lax.axis_index("blk")
    own_region = lax.dynamic_index_in_dim(region_of_block, position, 0, keepdims=False)
    row_ids = lax.broadcasted_iota(jnp.int32, (width, width), 0)
    col_ids = lax.broadcasted_iota(jnp.int32, (width, width), 1)
    tiles = [
        jnp.where(
            row_ids >= col_ids, factor_rows[:, :width], jnp.zeros((width, width), jnp.bfloat16)
        )
    ]
    valid = [None]
    for step in range(1, slots):
        tiles.append(factor_rows[:, step * width : (step + 1) * width])
        source = jnp.maximum(position - step, 0)
        source_region = lax.dynamic_index_in_dim(region_of_block, source, 0, keepdims=False)
        valid.append((position >= step) & (source_region == own_region))
    tables = filter_tables(time_kernel, FIRST)
    sources = lax.axis_size(("tm", "rep"))
    lifted = None
    for index, piece in enumerate(jnp.split(noise, CHUNKS, axis=1)):
        total = jnp.dot(tiles[0], piece, preferred_element_type=jnp.float32)
        carried = piece
        for step in range(1, slots):
            carried = shifted(carried, "blk", 1)
            if index == 0 and step == 1:
                tables, carried = lax.optimization_barrier((tables, carried))
            product = jnp.dot(tiles[step], carried, preferred_element_type=jnp.float32)
            total = total + jnp.where(valid[step], product, jnp.zeros_like(product))
        spatial = total.astype(jnp.bfloat16)
        regrouped = lax.all_to_all(spatial, ("tm", "rep"), split_axis=0, concat_axis=1, tiled=True)
        part = lift(tables, regrouped, sources, CHUNKS, index)
        lifted = part if lifted is None else lifted + part
    return filter_rest(tables, lifted, regrouped.shape[0])


def solution(mesh):
    placed = (P(("grp", "blk"), None), P(("grp", "blk"), ("tm", "rep")), P(), P("grp"))
    return jax.shard_map(
        on_device,
        mesh=mesh,
        in_specs=placed,
        out_specs=P(("grp", "blk", "tm", "rep"), None),
        check_vma=False,
    )
```

```python
import math

import jax
import jax.numpy as jnp
from jax import lax
from jax.experimental import pallas as pl
from jax.sharding import PartitionSpec as P

INTERPRET = False

FIRST = 64
CHUNKS = 4


def shifted(block, axis, distance):
    devices = range(lax.axis_size(axis))
    route = [(i - distance, i) for i in devices if i - distance in devices]
    return lax.ppermute(block, axis, route)


def filter_tables(time_kernel, first):
    second = time_kernel.shape[0] // first
    half = first // 2 + 1
    k = lax.broadcasted_iota(jnp.int32, (half, first), 0)
    a = lax.broadcasted_iota(jnp.int32, (half, first), 1)
    angle = 2.0 * math.pi / first * (k * a % first).astype(jnp.float32)
    cos_t = jnp.cos(angle)
    sin_t = jnp.sin(angle)
    taps = time_kernel.reshape(first, second)
    spec_re = jnp.dot(cos_t, taps, precision=lax.Precision.HIGHEST)
    spec_im = -jnp.dot(sin_t, taps, precision=lax.Precision.HIGHEST)
    turn = 2.0 * math.pi / first * jnp.arange(half, dtype=jnp.float32)
    cos_k = jnp.cos(turn)[:, None]
    sin_k = jnp.sin(turn)[:, None]
    ext_re = jnp.concatenate((spec_re, spec_re * cos_k + spec_im * sin_k), axis=1)
    ext_im = jnp.concatenate((spec_im, spec_im * cos_k - spec_re * sin_k), axis=1)

    ext = jnp.concatenate((ext_re, ext_im), axis=0)
    ext_hi = ext.astype(jnp.bfloat16)
    ext_lo = (ext - ext_hi.astype(jnp.float32)).astype(jnp.bfloat16)
    lag = lax.broadcasted_iota(jnp.int32, (2 * second, second, second), 0)
    row = lax.broadcasted_iota(jnp.int32, (2 * second, second, second), 1)
    col = lax.broadcasted_iota(jnp.int32, (2 * second, second, second), 2)
    pick = (lag == (col - row) % (2 * second)).astype(jnp.bfloat16)
    both = jnp.dot(
        jnp.concatenate((ext_hi, ext_lo), axis=0),
        pick.reshape(2 * second, second * second),
        preferred_element_type=jnp.float32,
    )
    mats = (both[: 2 * half] + both[2 * half :]).reshape(2 * half, second, second)

    forward = jnp.concatenate((cos_t, -sin_t), axis=0)
    forward_hi = forward.astype(jnp.bfloat16)
    forward_lo = (forward - forward_hi.astype(jnp.float32)).astype(jnp.bfloat16)
    weight = jnp.where((k[:, :1] == 0) | (k[:, :1] == first // 2), 1.0, 2.0) / first
    inv_re = jnp.transpose(cos_t * weight)
    inv_im = jnp.transpose(-sin_t * weight)
    return (mats.reshape(2, half, second, second), forward_hi, forward_lo, inv_re, inv_im)


def lift(tables, piece, sources, chunks, index):
    forward_hi, forward_lo = tables[1], tables[2]
    width, first = forward_hi.shape
    stations = piece.shape[0]
    second = piece.shape[1] // sources // (first // sources // chunks)
    rows = first // sources // chunks
    block = jnp.transpose(piece.reshape(stations, sources, rows, second), (1, 2, 0, 3))
    block = block.reshape(sources * rows, stations * second)

    def part(table):
        return table.reshape(width, sources, chunks, rows)[:, :, index, :].reshape(width, -1)

    return jnp.dot(part(forward_hi), block, preferred_element_type=jnp.float32) + jnp.dot(
        part(forward_lo), block, preferred_element_type=jnp.float32
    )


def mix_kernel(x_ref, m_ref, y_ref):
    def split(v):
        hi = v.astype(jnp.bfloat16)
        return hi, (v - hi.astype(jnp.float32)).astype(jnp.bfloat16)

    def dot3(u, m):
        u_hi, u_lo = split(u)
        m_hi, m_lo = split(m)
        total = jnp.dot(u_hi, m_hi, preferred_element_type=jnp.float32)
        total = total + jnp.dot(u_lo, m_hi, preferred_element_type=jnp.float32)
        return total + jnp.dot(u_hi, m_lo, preferred_element_type=jnp.float32)

    x_re = x_ref[0, 0]
    x_im = x_ref[1, 0]
    m_re = m_ref[0, 0]
    m_im = m_ref[1, 0]
    y_ref[0, 0] = dot3(x_re, m_re) - dot3(x_im, m_im)
    y_ref[1, 0] = dot3(x_re, m_im) + dot3(x_im, m_re)


def mix_all(lifted, mats, stations):
    half, second = mats.shape[1], mats.shape[2]
    x = lifted.reshape(2, half, stations, second)
    return pl.pallas_call(
        mix_kernel,
        grid=(half,),
        in_specs=[
            pl.BlockSpec((2, 1, stations, second), lambda k: (0, k, 0, 0)),
            pl.BlockSpec((2, 1, second, second), lambda k: (0, k, 0, 0)),
        ],
        out_specs=pl.BlockSpec((2, 1, stations, second), lambda k: (0, k, 0, 0)),
        out_shape=jax.ShapeDtypeStruct((2, half, stations, second), jnp.float32),
        interpret=INTERPRET,
    )(x, mats)


def filter_rest(tables, lifted, stations):
    mats, _, _, inv_re, inv_im = tables
    half, second = mats.shape[1], mats.shape[2]
    first = inv_re.shape[0]
    mixed = mix_all(lifted, mats, stations)
    y_re = mixed[0]
    y_im = mixed[1]
    out = jnp.dot(
        inv_re, y_re.reshape(half, stations * second), precision=lax.Precision.HIGH
    ) + jnp.dot(inv_im, y_im.reshape(half, stations * second), precision=lax.Precision.HIGH)
    out = out.astype(jnp.bfloat16).reshape(first, stations, second)
    return jnp.transpose(out, (1, 0, 2)).reshape(stations, first * second)


def on_device(factor_rows, noise, time_kernel, region_of_block):
    width = noise.shape[0]
    slots = factor_rows.shape[1] // width
    position = lax.axis_index("blk")
    own_region = lax.dynamic_index_in_dim(region_of_block, position, 0, keepdims=False)
    row_ids = lax.broadcasted_iota(jnp.int32, (width, width), 0)
    col_ids = lax.broadcasted_iota(jnp.int32, (width, width), 1)
    tiles = [
        jnp.where(
            row_ids >= col_ids, factor_rows[:, :width], jnp.zeros((width, width), jnp.bfloat16)
        )
    ]
    valid = [None]
    for step in range(1, slots):
        tiles.append(factor_rows[:, step * width : (step + 1) * width])
        source = jnp.maximum(position - step, 0)
        source_region = lax.dynamic_index_in_dim(region_of_block, source, 0, keepdims=False)
        valid.append((position >= step) & (source_region == own_region))
    tables = filter_tables(time_kernel, FIRST)
    sources = lax.axis_size(("tm", "rep"))
    lifted = None
    for index, piece in enumerate(jnp.split(noise, CHUNKS, axis=1)):
        total = jnp.dot(tiles[0], piece, preferred_element_type=jnp.float32)
        carried = piece
        for step in range(1, slots):
            carried = shifted(carried, "blk", 1)
            if index == 0 and step == 1:
                tables, carried = lax.optimization_barrier((tables, carried))
            product = jnp.dot(tiles[step], carried, preferred_element_type=jnp.float32)
            total = total + jnp.where(valid[step], product, jnp.zeros_like(product))
        spatial = total.astype(jnp.bfloat16)
        regrouped = lax.all_to_all(spatial, ("tm", "rep"), split_axis=0, concat_axis=1, tiled=True)
        part = lift(tables, regrouped, sources, CHUNKS, index)
        lifted = part if lifted is None else lifted + part
    return filter_rest(tables, lifted, regrouped.shape[0])


def solution(mesh):
    placed = (P(("grp", "blk"), None), P(("grp", "blk"), ("tm", "rep")), P(), P("grp"))
    return jax.shard_map(
        on_device,
        mesh=mesh,
        in_specs=placed,
        out_specs=P(("grp", "blk", "tm", "rep"), None),
        check_vma=False,
    )
```

```python
import math

import jax
import jax.numpy as jnp
from jax import lax
from jax.sharding import PartitionSpec as P

FIRST = 64
CHUNKS = 4


def shifted(block, axis, distance):
    devices = range(lax.axis_size(axis))
    route = [(i - distance, i) for i in devices if i - distance in devices]
    return lax.ppermute(block, axis, route)


def filter_tables(time_kernel, first):
    second = time_kernel.shape[0] // first
    half = first // 2 + 1
    k = lax.broadcasted_iota(jnp.int32, (half, first), 0)
    a = lax.broadcasted_iota(jnp.int32, (half, first), 1)
    angle = 2.0 * math.pi / first * (k * a % first).astype(jnp.float32)
    cos_t = jnp.cos(angle)
    sin_t = jnp.sin(angle)
    taps = time_kernel.reshape(first, second)
    spec_re = jnp.dot(cos_t, taps, precision=lax.Precision.HIGHEST)
    spec_im = -jnp.dot(sin_t, taps, precision=lax.Precision.HIGHEST)
    turn = 2.0 * math.pi / first * jnp.arange(half, dtype=jnp.float32)
    cos_k = jnp.cos(turn)[:, None]
    sin_k = jnp.sin(turn)[:, None]
    ext_re = jnp.concatenate((spec_re, spec_re * cos_k + spec_im * sin_k), axis=1)
    ext_im = jnp.concatenate((spec_im, spec_im * cos_k - spec_re * sin_k), axis=1)

    ext = jnp.concatenate((ext_re, ext_im), axis=0)
    ext_hi = ext.astype(jnp.bfloat16)
    ext_lo = (ext - ext_hi.astype(jnp.float32)).astype(jnp.bfloat16)
    lag = lax.broadcasted_iota(jnp.int32, (2 * second, second, second), 0)
    row = lax.broadcasted_iota(jnp.int32, (2 * second, second, second), 1)
    col = lax.broadcasted_iota(jnp.int32, (2 * second, second, second), 2)
    pick = (lag == (col - row) % (2 * second)).astype(jnp.bfloat16)
    both = jnp.dot(
        jnp.concatenate((ext_hi, ext_lo), axis=0),
        pick.reshape(2 * second, second * second),
        preferred_element_type=jnp.float32,
    )
    mats = (both[: 2 * half] + both[2 * half :]).reshape(2 * half, second, second)

    forward = jnp.concatenate((cos_t, -sin_t), axis=0)
    forward_hi = forward.astype(jnp.bfloat16)
    forward_lo = (forward - forward_hi.astype(jnp.float32)).astype(jnp.bfloat16)
    weight = jnp.where((k[:, :1] == 0) | (k[:, :1] == first // 2), 1.0, 2.0) / first
    inv_re = jnp.transpose(cos_t * weight)
    inv_im = jnp.transpose(-sin_t * weight)
    return (mats[:half], mats[half:], forward_hi, forward_lo, inv_re, inv_im)


def filter_rest(tables, lifted, stations):
    mat_re, mat_im, _, _, inv_re, inv_im = tables
    half, second = mat_re.shape[0], mat_re.shape[1]
    first = inv_re.shape[0]
    x_re = lifted[:half].reshape(half, stations, second)
    x_im = lifted[half:].reshape(half, stations, second)

    def mix(u, m):
        return jnp.einsum(
            "ksc,kcd->ksd", u, m,
            precision=lax.Precision.HIGH, preferred_element_type=jnp.float32,
        )

    y_re = mix(x_re, mat_re) - mix(x_im, mat_im)
    y_im = mix(x_re, mat_im) + mix(x_im, mat_re)
    out = jnp.dot(
        inv_re, y_re.reshape(half, stations * second), precision=lax.Precision.HIGH
    ) + jnp.dot(inv_im, y_im.reshape(half, stations * second), precision=lax.Precision.HIGH)
    out = out.astype(jnp.bfloat16).reshape(first, stations, second)
    return jnp.transpose(out, (1, 0, 2)).reshape(stations, first * second)


def on_device(factor_rows, noise, time_kernel, region_of_block):
    width = noise.shape[0]
    slots = factor_rows.shape[1] // width
    position = lax.axis_index("blk")
    own_region = lax.dynamic_index_in_dim(region_of_block, position, 0, keepdims=False)
    row_ids = lax.broadcasted_iota(jnp.int32, (width, width), 0)
    col_ids = lax.broadcasted_iota(jnp.int32, (width, width), 1)
    tiles = [
        jnp.where(
            row_ids >= col_ids, factor_rows[:, :width], jnp.zeros((width, width), jnp.bfloat16)
        )
    ]
    valid = [None]
    for step in range(1, slots):
        tiles.append(factor_rows[:, step * width : (step + 1) * width])
        source = jnp.maximum(position - step, 0)
        source_region = lax.dynamic_index_in_dim(region_of_block, source, 0, keepdims=False)
        valid.append((position >= step) & (source_region == own_region))
    tables = filter_tables(time_kernel, FIRST)
    sources = lax.axis_size(("tm", "rep"))
    pieces = []
    for index, piece in enumerate(jnp.split(noise, CHUNKS, axis=1)):
        total = jnp.dot(tiles[0], piece, preferred_element_type=jnp.float32)
        carried = piece
        for step in range(1, slots):
            carried = shifted(carried, "blk", 1)
            if index == 0 and step == 1:
                tables, carried = lax.optimization_barrier((tables, carried))
            product = jnp.dot(tiles[step], carried, preferred_element_type=jnp.float32)
            total = total + jnp.where(valid[step], product, jnp.zeros_like(product))
        spatial = total.astype(jnp.bfloat16)
        second = time_kernel.shape[0] // FIRST
        rows = spatial.shape[1] // second
        spatial = jnp.transpose(spatial.reshape(width, rows, second), (1, 0, 2))
        pieces.append(
            lax.all_to_all(spatial, ("tm", "rep"), split_axis=1, concat_axis=0, tiled=True)
        )
    grid = jnp.concatenate(pieces, axis=0)
    stations = grid.shape[1]

    def order(table):
        return jnp.transpose(
            table.reshape(table.shape[0], sources, CHUNKS, rows), (0, 2, 1, 3)
        ).reshape(table.shape[0], -1)

    flat = grid.reshape(grid.shape[0], stations * second)
    lifted = jnp.dot(order(tables[2]), flat, preferred_element_type=jnp.float32) + jnp.dot(
        order(tables[3]), flat, preferred_element_type=jnp.float32
    )
    return filter_rest(tables, lifted, stations)


def solution(mesh):
    placed = (P(("grp", "blk"), None), P(("grp", "blk"), ("tm", "rep")), P(), P("grp"))
    return jax.shard_map(
        on_device,
        mesh=mesh,
        in_specs=placed,
        out_specs=P(("grp", "blk", "tm", "rep"), None),
        check_vma=False,
    )
```

```python
import math

import jax
import jax.numpy as jnp
from jax import lax
from jax.sharding import PartitionSpec as P

FIRST = 64
CHUNKS = 4


def shifted(block, axis, distance):
    devices = range(lax.axis_size(axis))
    route = [(i - distance, i) for i in devices if i - distance in devices]
    return lax.ppermute(block, axis, route)


def filter_tables(time_kernel, first):
    second = time_kernel.shape[0] // first
    half = first // 2 + 1
    k = lax.broadcasted_iota(jnp.int32, (half, first), 0)
    a = lax.broadcasted_iota(jnp.int32, (half, first), 1)
    angle = 2.0 * math.pi / first * (k * a % first).astype(jnp.float32)
    cos_t = jnp.cos(angle)
    sin_t = jnp.sin(angle)
    taps = time_kernel.reshape(first, second)
    spec_re = jnp.dot(cos_t, taps, precision=lax.Precision.HIGHEST)
    spec_im = -jnp.dot(sin_t, taps, precision=lax.Precision.HIGHEST)
    turn = 2.0 * math.pi / first * jnp.arange(half, dtype=jnp.float32)
    cos_k = jnp.cos(turn)[:, None]
    sin_k = jnp.sin(turn)[:, None]
    ext_re = jnp.concatenate((spec_re, spec_re * cos_k + spec_im * sin_k), axis=1)
    ext_im = jnp.concatenate((spec_im, spec_im * cos_k - spec_re * sin_k), axis=1)

    ext = jnp.concatenate((ext_re, ext_im), axis=0)
    ext_hi = ext.astype(jnp.bfloat16)
    ext_lo = (ext - ext_hi.astype(jnp.float32)).astype(jnp.bfloat16)
    lag = lax.broadcasted_iota(jnp.int32, (2 * second, second, second), 0)
    row = lax.broadcasted_iota(jnp.int32, (2 * second, second, second), 1)
    col = lax.broadcasted_iota(jnp.int32, (2 * second, second, second), 2)
    pick = (lag == (col - row) % (2 * second)).astype(jnp.bfloat16)
    both = jnp.dot(
        jnp.concatenate((ext_hi, ext_lo), axis=0),
        pick.reshape(2 * second, second * second),
        preferred_element_type=jnp.float32,
    )
    mats = (both[: 2 * half] + both[2 * half :]).reshape(2 * half, second, second)

    forward = jnp.concatenate((cos_t, -sin_t), axis=0)
    forward_hi = forward.astype(jnp.bfloat16)
    forward_lo = (forward - forward_hi.astype(jnp.float32)).astype(jnp.bfloat16)
    weight = jnp.where((k[:, :1] == 0) | (k[:, :1] == first // 2), 1.0, 2.0) / first
    inv_re = jnp.transpose(cos_t * weight)
    inv_im = jnp.transpose(-sin_t * weight)
    return (mats[:half], mats[half:], forward_hi, forward_lo, inv_re, inv_im)


def filter_rest(tables, lifted, stations):
    mat_re, mat_im, _, _, inv_re, inv_im = tables
    half, second = mat_re.shape[0], mat_re.shape[1]
    first = inv_re.shape[0]
    x_re = lifted[:half].reshape(half, stations, second)
    x_im = lifted[half:].reshape(half, stations, second)

    def mix(u, m):
        return jnp.einsum(
            "ksc,kcd->ksd", u, m,
            precision=lax.Precision.HIGH, preferred_element_type=jnp.float32,
        )

    y_re = mix(x_re, mat_re) - mix(x_im, mat_im)
    y_im = mix(x_re, mat_im) + mix(x_im, mat_re)
    out = jnp.dot(
        inv_re, y_re.reshape(half, stations * second), precision=lax.Precision.HIGH
    ) + jnp.dot(inv_im, y_im.reshape(half, stations * second), precision=lax.Precision.HIGH)
    out = out.astype(jnp.bfloat16).reshape(first, stations, second)
    return jnp.transpose(out, (1, 0, 2)).reshape(stations, first * second)


def on_device(factor_rows, noise, time_kernel, region_of_block):
    width = noise.shape[0]
    slots = factor_rows.shape[1] // width
    position = lax.axis_index("blk")
    own_region = lax.dynamic_index_in_dim(region_of_block, position, 0, keepdims=False)
    row_ids = lax.broadcasted_iota(jnp.int32, (width, width), 0)
    col_ids = lax.broadcasted_iota(jnp.int32, (width, width), 1)
    tiles = [
        jnp.where(
            row_ids >= col_ids, factor_rows[:, :width], jnp.zeros((width, width), jnp.bfloat16)
        )
    ]
    valid = [None]
    for step in range(1, slots):
        tiles.append(factor_rows[:, step * width : (step + 1) * width])
        source = jnp.maximum(position - step, 0)
        source_region = lax.dynamic_index_in_dim(region_of_block, source, 0, keepdims=False)
        valid.append((position >= step) & (source_region == own_region))
    tables = filter_tables(time_kernel, FIRST)
    sources = lax.axis_size(("tm", "rep"))
    pieces = []
    gate = None
    for index, piece in enumerate(jnp.split(noise, CHUNKS, axis=1)):
        if gate is not None:
            piece, gate = lax.optimization_barrier((piece, gate))
        total = jnp.dot(tiles[0], piece, preferred_element_type=jnp.float32)
        carried = piece
        for step in range(1, slots):
            carried = shifted(carried, "blk", 1)
            if index == 0 and step == 1:
                tables, carried = lax.optimization_barrier((tables, carried))
            if step == min(2, slots - 1):
                gate = carried
            product = jnp.dot(tiles[step], carried, preferred_element_type=jnp.float32)
            total = total + jnp.where(valid[step], product, jnp.zeros_like(product))
        spatial = total.astype(jnp.bfloat16)
        second = time_kernel.shape[0] // FIRST
        rows = spatial.shape[1] // second
        spatial = jnp.transpose(spatial.reshape(width, rows, second), (1, 0, 2))
        pieces.append(
            lax.all_to_all(spatial, ("tm", "rep"), split_axis=1, concat_axis=0, tiled=True)
        )
    grid = jnp.concatenate(pieces, axis=0)
    stations = grid.shape[1]

    def order(table):
        return jnp.transpose(
            table.reshape(table.shape[0], sources, CHUNKS, rows), (0, 2, 1, 3)
        ).reshape(table.shape[0], -1)

    flat = grid.reshape(grid.shape[0], stations * second)
    lifted = jnp.dot(order(tables[2]), flat, preferred_element_type=jnp.float32) + jnp.dot(
        order(tables[3]), flat, preferred_element_type=jnp.float32
    )
    return filter_rest(tables, lifted, stations)


def solution(mesh):
    placed = (P(("grp", "blk"), None), P(("grp", "blk"), ("tm", "rep")), P(), P("grp"))
    return jax.shard_map(
        on_device,
        mesh=mesh,
        in_specs=placed,
        out_specs=P(("grp", "blk", "tm", "rep"), None),
        check_vma=False,
    )
```

```python
import math

import jax
import jax.numpy as jnp
from jax import lax
from jax.sharding import PartitionSpec as P

FIRST = 64
CHUNKS = 2


def shifted(block, axis, distance):
    devices = range(lax.axis_size(axis))
    route = [(i - distance, i) for i in devices if i - distance in devices]
    return lax.ppermute(block, axis, route)


def filter_tables(time_kernel, first):
    second = time_kernel.shape[0] // first
    half = first // 2 + 1
    k = lax.broadcasted_iota(jnp.int32, (half, first), 0)
    a = lax.broadcasted_iota(jnp.int32, (half, first), 1)
    angle = 2.0 * math.pi / first * (k * a % first).astype(jnp.float32)
    cos_t = jnp.cos(angle)
    sin_t = jnp.sin(angle)
    taps = time_kernel.reshape(first, second)
    spec_re = jnp.dot(cos_t, taps, precision=lax.Precision.HIGHEST)
    spec_im = -jnp.dot(sin_t, taps, precision=lax.Precision.HIGHEST)
    turn = 2.0 * math.pi / first * jnp.arange(half, dtype=jnp.float32)
    cos_k = jnp.cos(turn)[:, None]
    sin_k = jnp.sin(turn)[:, None]
    ext_re = jnp.concatenate((spec_re, spec_re * cos_k + spec_im * sin_k), axis=1)
    ext_im = jnp.concatenate((spec_im, spec_im * cos_k - spec_re * sin_k), axis=1)

    ext = jnp.concatenate((ext_re, ext_im), axis=0)
    ext_hi = ext.astype(jnp.bfloat16)
    ext_lo = (ext - ext_hi.astype(jnp.float32)).astype(jnp.bfloat16)
    lag = lax.broadcasted_iota(jnp.int32, (2 * second, second, second), 0)
    row = lax.broadcasted_iota(jnp.int32, (2 * second, second, second), 1)
    col = lax.broadcasted_iota(jnp.int32, (2 * second, second, second), 2)
    pick = (lag == (col - row) % (2 * second)).astype(jnp.bfloat16)
    both = jnp.dot(
        jnp.concatenate((ext_hi, ext_lo), axis=0),
        pick.reshape(2 * second, second * second),
        preferred_element_type=jnp.float32,
    )
    mats = (both[: 2 * half] + both[2 * half :]).reshape(2 * half, second, second)

    forward = jnp.concatenate((cos_t, -sin_t), axis=0)
    forward_hi = forward.astype(jnp.bfloat16)
    forward_lo = (forward - forward_hi.astype(jnp.float32)).astype(jnp.bfloat16)
    weight = jnp.where((k[:, :1] == 0) | (k[:, :1] == first // 2), 1.0, 2.0) / first
    inv_re = jnp.transpose(cos_t * weight)
    inv_im = jnp.transpose(-sin_t * weight)
    return (mats[:half], mats[half:], forward_hi, forward_lo, inv_re, inv_im)


def filter_rest(tables, lifted, stations):
    mat_re, mat_im, _, _, inv_re, inv_im = tables
    half, second = mat_re.shape[0], mat_re.shape[1]
    first = inv_re.shape[0]
    x_re = lifted[:half].reshape(half, stations, second)
    x_im = lifted[half:].reshape(half, stations, second)

    def mix(u, m):
        return jnp.einsum(
            "ksc,kcd->ksd", u, m,
            precision=lax.Precision.HIGH, preferred_element_type=jnp.float32,
        )

    y_re = mix(x_re, mat_re) - mix(x_im, mat_im)
    y_im = mix(x_re, mat_im) + mix(x_im, mat_re)
    out = jnp.dot(
        inv_re, y_re.reshape(half, stations * second), precision=lax.Precision.HIGH
    ) + jnp.dot(inv_im, y_im.reshape(half, stations * second), precision=lax.Precision.HIGH)
    out = out.astype(jnp.bfloat16).reshape(first, stations, second)
    return jnp.transpose(out, (1, 0, 2)).reshape(stations, first * second)


def on_device(factor_rows, noise, time_kernel, region_of_block):
    width = noise.shape[0]
    slots = factor_rows.shape[1] // width
    position = lax.axis_index("blk")
    own_region = lax.dynamic_index_in_dim(region_of_block, position, 0, keepdims=False)
    row_ids = lax.broadcasted_iota(jnp.int32, (width, width), 0)
    col_ids = lax.broadcasted_iota(jnp.int32, (width, width), 1)
    tiles = [
        jnp.where(
            row_ids >= col_ids, factor_rows[:, :width], jnp.zeros((width, width), jnp.bfloat16)
        )
    ]
    valid = [None]
    for step in range(1, slots):
        tiles.append(factor_rows[:, step * width : (step + 1) * width])
        source = jnp.maximum(position - step, 0)
        source_region = lax.dynamic_index_in_dim(region_of_block, source, 0, keepdims=False)
        valid.append((position >= step) & (source_region == own_region))
    tables = filter_tables(time_kernel, FIRST)
    sources = lax.axis_size(("tm", "rep"))
    pieces = []
    for index, piece in enumerate(jnp.split(noise, CHUNKS, axis=1)):
        total = jnp.dot(tiles[0], piece, preferred_element_type=jnp.float32)
        carried = piece
        for step in range(1, slots):
            carried = shifted(carried, "blk", 1)
            if index == 0 and step == 1:
                tables, carried = lax.optimization_barrier((tables, carried))
            product = jnp.dot(tiles[step], carried, preferred_element_type=jnp.float32)
            total = total + jnp.where(valid[step], product, jnp.zeros_like(product))
        spatial = total.astype(jnp.bfloat16)
        second = time_kernel.shape[0] // FIRST
        rows = spatial.shape[1] // second
        spatial = jnp.transpose(spatial.reshape(width, rows, second), (1, 0, 2))
        pieces.append(
            lax.all_to_all(spatial, ("tm", "rep"), split_axis=1, concat_axis=0, tiled=True)
        )
    grid = jnp.concatenate(pieces, axis=0)
    stations = grid.shape[1]

    def order(table):
        return jnp.transpose(
            table.reshape(table.shape[0], sources, CHUNKS, rows), (0, 2, 1, 3)
        ).reshape(table.shape[0], -1)

    flat = grid.reshape(grid.shape[0], stations * second)
    lifted = jnp.dot(order(tables[2]), flat, preferred_element_type=jnp.float32) + jnp.dot(
        order(tables[3]), flat, preferred_element_type=jnp.float32
    )
    return filter_rest(tables, lifted, stations)


def solution(mesh):
    placed = (P(("grp", "blk"), None), P(("grp", "blk"), ("tm", "rep")), P(), P("grp"))
    return jax.shard_map(
        on_device,
        mesh=mesh,
        in_specs=placed,
        out_specs=P(("grp", "blk", "tm", "rep"), None),
        check_vma=False,
    )
```

```python
import math

import jax
import jax.numpy as jnp
from jax import lax
from jax.sharding import PartitionSpec as P

FIRST = 64
CHUNKS = 1


def shifted(block, axis, distance):
    devices = range(lax.axis_size(axis))
    route = [(i - distance, i) for i in devices if i - distance in devices]
    return lax.ppermute(block, axis, route)


def filter_tables(time_kernel, first):
    second = time_kernel.shape[0] // first
    half = first // 2 + 1
    k = lax.broadcasted_iota(jnp.int32, (half, first), 0)
    a = lax.broadcasted_iota(jnp.int32, (half, first), 1)
    angle = 2.0 * math.pi / first * (k * a % first).astype(jnp.float32)
    cos_t = jnp.cos(angle)
    sin_t = jnp.sin(angle)
    taps = time_kernel.reshape(first, second)
    spec_re = jnp.dot(cos_t, taps, precision=lax.Precision.HIGHEST)
    spec_im = -jnp.dot(sin_t, taps, precision=lax.Precision.HIGHEST)
    turn = 2.0 * math.pi / first * jnp.arange(half, dtype=jnp.float32)
    cos_k = jnp.cos(turn)[:, None]
    sin_k = jnp.sin(turn)[:, None]
    ext_re = jnp.concatenate((spec_re, spec_re * cos_k + spec_im * sin_k), axis=1)
    ext_im = jnp.concatenate((spec_im, spec_im * cos_k - spec_re * sin_k), axis=1)

    ext = jnp.concatenate((ext_re, ext_im), axis=0)
    ext_hi = ext.astype(jnp.bfloat16)
    ext_lo = (ext - ext_hi.astype(jnp.float32)).astype(jnp.bfloat16)
    lag = lax.broadcasted_iota(jnp.int32, (2 * second, second, second), 0)
    row = lax.broadcasted_iota(jnp.int32, (2 * second, second, second), 1)
    col = lax.broadcasted_iota(jnp.int32, (2 * second, second, second), 2)
    pick = (lag == (col - row) % (2 * second)).astype(jnp.bfloat16)
    both = jnp.dot(
        jnp.concatenate((ext_hi, ext_lo), axis=0),
        pick.reshape(2 * second, second * second),
        preferred_element_type=jnp.float32,
    )
    mats = (both[: 2 * half] + both[2 * half :]).reshape(2 * half, second, second)

    forward = jnp.concatenate((cos_t, -sin_t), axis=0)
    forward_hi = forward.astype(jnp.bfloat16)
    forward_lo = (forward - forward_hi.astype(jnp.float32)).astype(jnp.bfloat16)
    weight = jnp.where((k[:, :1] == 0) | (k[:, :1] == first // 2), 1.0, 2.0) / first
    inv_re = jnp.transpose(cos_t * weight)
    inv_im = jnp.transpose(-sin_t * weight)
    return (mats[:half], mats[half:], forward_hi, forward_lo, inv_re, inv_im)


def filter_rest(tables, lifted, stations):
    mat_re, mat_im, _, _, inv_re, inv_im = tables
    half, second = mat_re.shape[0], mat_re.shape[1]
    first = inv_re.shape[0]
    x_re = lifted[:half].reshape(half, stations, second)
    x_im = lifted[half:].reshape(half, stations, second)

    def mix(u, m):
        return jnp.einsum(
            "ksc,kcd->ksd", u, m,
            precision=lax.Precision.HIGH, preferred_element_type=jnp.float32,
        )

    y_re = mix(x_re, mat_re) - mix(x_im, mat_im)
    y_im = mix(x_re, mat_im) + mix(x_im, mat_re)
    out = jnp.dot(
        inv_re, y_re.reshape(half, stations * second), precision=lax.Precision.HIGH
    ) + jnp.dot(inv_im, y_im.reshape(half, stations * second), precision=lax.Precision.HIGH)
    out = out.astype(jnp.bfloat16).reshape(first, stations, second)
    return jnp.transpose(out, (1, 0, 2)).reshape(stations, first * second)


def on_device(factor_rows, noise, time_kernel, region_of_block):
    width = noise.shape[0]
    slots = factor_rows.shape[1] // width
    position = lax.axis_index("blk")
    own_region = lax.dynamic_index_in_dim(region_of_block, position, 0, keepdims=False)
    row_ids = lax.broadcasted_iota(jnp.int32, (width, width), 0)
    col_ids = lax.broadcasted_iota(jnp.int32, (width, width), 1)
    tiles = [
        jnp.where(
            row_ids >= col_ids, factor_rows[:, :width], jnp.zeros((width, width), jnp.bfloat16)
        )
    ]
    valid = [None]
    for step in range(1, slots):
        tiles.append(factor_rows[:, step * width : (step + 1) * width])
        source = jnp.maximum(position - step, 0)
        source_region = lax.dynamic_index_in_dim(region_of_block, source, 0, keepdims=False)
        valid.append((position >= step) & (source_region == own_region))
    tables = filter_tables(time_kernel, FIRST)
    sources = lax.axis_size(("tm", "rep"))
    pieces = []
    for index, piece in enumerate(jnp.split(noise, CHUNKS, axis=1)):
        total = jnp.dot(tiles[0], piece, preferred_element_type=jnp.float32)
        carried = piece
        for step in range(1, slots):
            carried = shifted(carried, "blk", 1)
            if index == 0 and step == 1:
                tables, carried = lax.optimization_barrier((tables, carried))
            product = jnp.dot(tiles[step], carried, preferred_element_type=jnp.float32)
            total = total + jnp.where(valid[step], product, jnp.zeros_like(product))
        spatial = total.astype(jnp.bfloat16)
        second = time_kernel.shape[0] // FIRST
        rows = spatial.shape[1] // second
        spatial = jnp.transpose(spatial.reshape(width, rows, second), (1, 0, 2))
        pieces.append(
            lax.all_to_all(spatial, ("tm", "rep"), split_axis=1, concat_axis=0, tiled=True)
        )
    grid = jnp.concatenate(pieces, axis=0)
    stations = grid.shape[1]

    def order(table):
        return jnp.transpose(
            table.reshape(table.shape[0], sources, CHUNKS, rows), (0, 2, 1, 3)
        ).reshape(table.shape[0], -1)

    flat = grid.reshape(grid.shape[0], stations * second)
    lifted = jnp.dot(order(tables[2]), flat, preferred_element_type=jnp.float32) + jnp.dot(
        order(tables[3]), flat, preferred_element_type=jnp.float32
    )
    return filter_rest(tables, lifted, stations)


def solution(mesh):
    placed = (P(("grp", "blk"), None), P(("grp", "blk"), ("tm", "rep")), P(), P("grp"))
    return jax.shard_map(
        on_device,
        mesh=mesh,
        in_specs=placed,
        out_specs=P(("grp", "blk", "tm", "rep"), None),
        check_vma=False,
    )
```

```python
import math

import jax
import jax.numpy as jnp
from jax import lax
from jax.sharding import PartitionSpec as P

FIRST = 64
CHUNKS = 2


def shifted(block, axis, distance):
    devices = range(lax.axis_size(axis))
    route = [(i - distance, i) for i in devices if i - distance in devices]
    return lax.ppermute(block, axis, route)


def filter_tables(time_kernel, first):
    second = time_kernel.shape[0] // first
    half = first // 2 + 1
    k = lax.broadcasted_iota(jnp.int32, (half, first), 0)
    a = lax.broadcasted_iota(jnp.int32, (half, first), 1)
    angle = 2.0 * math.pi / first * (k * a % first).astype(jnp.float32)
    cos_t = jnp.cos(angle)
    sin_t = jnp.sin(angle)
    taps = time_kernel.reshape(first, second)
    spec_re = jnp.dot(cos_t, taps, precision=lax.Precision.HIGHEST)
    spec_im = -jnp.dot(sin_t, taps, precision=lax.Precision.HIGHEST)
    turn = 2.0 * math.pi / first * jnp.arange(half, dtype=jnp.float32)
    cos_k = jnp.cos(turn)[:, None]
    sin_k = jnp.sin(turn)[:, None]
    ext_re = jnp.concatenate((spec_re, spec_re * cos_k + spec_im * sin_k), axis=1)
    ext_im = jnp.concatenate((spec_im, spec_im * cos_k - spec_re * sin_k), axis=1)

    ext = jnp.concatenate((ext_re, ext_im), axis=0)
    ext_hi = ext.astype(jnp.bfloat16)
    ext_lo = (ext - ext_hi.astype(jnp.float32)).astype(jnp.bfloat16)
    lag = lax.broadcasted_iota(jnp.int32, (2 * second, second, second), 0)
    row = lax.broadcasted_iota(jnp.int32, (2 * second, second, second), 1)
    col = lax.broadcasted_iota(jnp.int32, (2 * second, second, second), 2)
    pick = (lag == (col - row) % (2 * second)).astype(jnp.bfloat16)
    both = jnp.dot(
        jnp.concatenate((ext_hi, ext_lo), axis=0),
        pick.reshape(2 * second, second * second),
        preferred_element_type=jnp.float32,
    )
    mats = (both[: 2 * half] + both[2 * half :]).reshape(2 * half, second, second)

    forward = jnp.concatenate((cos_t, -sin_t), axis=0)
    forward_hi = forward.astype(jnp.bfloat16)
    forward_lo = (forward - forward_hi.astype(jnp.float32)).astype(jnp.bfloat16)
    weight = jnp.where((k[:, :1] == 0) | (k[:, :1] == first // 2), 1.0, 2.0) / first
    inv_re = jnp.transpose(cos_t * weight)
    inv_im = jnp.transpose(-sin_t * weight)
    return (mats[:half], mats[half:], forward_hi, forward_lo, inv_re, inv_im)


def filter_rest(tables, lifted, stations):
    mat_re, mat_im, _, _, inv_re, inv_im = tables
    half, second = mat_re.shape[0], mat_re.shape[1]
    first = inv_re.shape[0]
    x_re = lifted[:half].reshape(half, stations, second)
    x_im = lifted[half:].reshape(half, stations, second)

    def mix(u, m):
        return jnp.einsum(
            "ksc,kcd->ksd", u, m,
            precision=lax.Precision.HIGH, preferred_element_type=jnp.float32,
        )

    y_re = mix(x_re, mat_re) - mix(x_im, mat_im)
    y_im = mix(x_re, mat_im) + mix(x_im, mat_re)
    out = jnp.dot(
        inv_re, y_re.reshape(half, stations * second), precision=lax.Precision.HIGH
    ) + jnp.dot(inv_im, y_im.reshape(half, stations * second), precision=lax.Precision.HIGH)
    out = out.astype(jnp.bfloat16).reshape(first, stations, second)
    return jnp.transpose(out, (1, 0, 2)).reshape(stations, first * second)


def exchange(block, sources, me):
    width = block.shape[1] // sources
    out = []
    for step in range(sources):
        target = (me + step) % sources
        part = lax.dynamic_slice_in_dim(block, target * width, width, 1)
        if step:
            route = [(i, (i + step) % sources) for i in range(sources)]
            part = lax.ppermute(part, ("tm", "rep"), route)
        out.append(part)
    return out


def on_device(factor_rows, noise, time_kernel, region_of_block):
    width = noise.shape[0]
    slots = factor_rows.shape[1] // width
    position = lax.axis_index("blk")
    own_region = lax.dynamic_index_in_dim(region_of_block, position, 0, keepdims=False)
    row_ids = lax.broadcasted_iota(jnp.int32, (width, width), 0)
    col_ids = lax.broadcasted_iota(jnp.int32, (width, width), 1)
    tiles = [
        jnp.where(
            row_ids >= col_ids, factor_rows[:, :width], jnp.zeros((width, width), jnp.bfloat16)
        )
    ]
    valid = [None]
    for step in range(1, slots):
        tiles.append(factor_rows[:, step * width : (step + 1) * width])
        source = jnp.maximum(position - step, 0)
        source_region = lax.dynamic_index_in_dim(region_of_block, source, 0, keepdims=False)
        valid.append((position >= step) & (source_region == own_region))
    tables = filter_tables(time_kernel, FIRST)
    sources = lax.axis_size(("tm", "rep"))
    me = lax.axis_index(("tm", "rep"))
    pieces = []
    for index, piece in enumerate(jnp.split(noise, CHUNKS, axis=1)):
        total = jnp.dot(tiles[0], piece, preferred_element_type=jnp.float32)
        carried = piece
        for step in range(1, slots):
            carried = shifted(carried, "blk", 1)
            if index == 0 and step == 1:
                tables, carried = lax.optimization_barrier((tables, carried))
            product = jnp.dot(tiles[step], carried, preferred_element_type=jnp.float32)
            total = total + jnp.where(valid[step], product, jnp.zeros_like(product))
        spatial = total.astype(jnp.bfloat16)
        second = time_kernel.shape[0] // FIRST
        rows = spatial.shape[1] // second
        spatial = jnp.transpose(spatial.reshape(width, rows, second), (1, 0, 2))
        pieces.extend(exchange(spatial, sources, me))
    grid = jnp.concatenate(pieces, axis=0)
    stations = grid.shape[1]

    def order(table):
        blocks = table.reshape(table.shape[0], sources, CHUNKS, rows)[:, ::-1]
        blocks = jnp.roll(blocks, me + 1 - sources, axis=1)
        return jnp.transpose(blocks, (0, 2, 1, 3)).reshape(table.shape[0], -1)

    flat = grid.reshape(grid.shape[0], stations * second)
    lifted = jnp.dot(order(tables[2]), flat, preferred_element_type=jnp.float32) + jnp.dot(
        order(tables[3]), flat, preferred_element_type=jnp.float32
    )
    return filter_rest(tables, lifted, stations)


def solution(mesh):
    placed = (P(("grp", "blk"), None), P(("grp", "blk"), ("tm", "rep")), P(), P("grp"))
    return jax.shard_map(
        on_device,
        mesh=mesh,
        in_specs=placed,
        out_specs=P(("grp", "blk", "tm", "rep"), None),
        check_vma=False,
    )
```

```python
import math

import jax
import jax.numpy as jnp
from jax import lax
from jax.sharding import PartitionSpec as P

FIRST = 64
CHUNKS = 4


def shifted(block, axis, distance):
    devices = range(lax.axis_size(axis))
    route = [(i - distance, i) for i in devices if i - distance in devices]
    return lax.ppermute(block, axis, route)


def filter_tables(time_kernel, first):
    second = time_kernel.shape[0] // first
    half = first // 2 + 1
    k = lax.broadcasted_iota(jnp.int32, (half, first), 0)
    a = lax.broadcasted_iota(jnp.int32, (half, first), 1)
    angle = 2.0 * math.pi / first * (k * a % first).astype(jnp.float32)
    cos_t = jnp.cos(angle)
    sin_t = jnp.sin(angle)
    taps = time_kernel.reshape(first, second)
    spec_re = jnp.dot(cos_t, taps, precision=lax.Precision.HIGHEST)
    spec_im = -jnp.dot(sin_t, taps, precision=lax.Precision.HIGHEST)
    turn = 2.0 * math.pi / first * jnp.arange(half, dtype=jnp.float32)
    cos_k = jnp.cos(turn)[:, None]
    sin_k = jnp.sin(turn)[:, None]
    ext_re = jnp.concatenate((spec_re, spec_re * cos_k + spec_im * sin_k), axis=1)
    ext_im = jnp.concatenate((spec_im, spec_im * cos_k - spec_re * sin_k), axis=1)

    ext = jnp.concatenate((ext_re, ext_im), axis=0)
    ext_hi = ext.astype(jnp.bfloat16)
    ext_lo = (ext - ext_hi.astype(jnp.float32)).astype(jnp.bfloat16)
    lag = lax.broadcasted_iota(jnp.int32, (2 * second, second, second), 0)
    row = lax.broadcasted_iota(jnp.int32, (2 * second, second, second), 1)
    col = lax.broadcasted_iota(jnp.int32, (2 * second, second, second), 2)
    pick = (lag == (col - row) % (2 * second)).astype(jnp.bfloat16)
    both = jnp.dot(
        jnp.concatenate((ext_hi, ext_lo), axis=0),
        pick.reshape(2 * second, second * second),
        preferred_element_type=jnp.float32,
    )
    mats = (both[: 2 * half] + both[2 * half :]).reshape(2 * half, second, second)

    forward = jnp.concatenate((cos_t, -sin_t), axis=0)
    forward_hi = forward.astype(jnp.bfloat16)
    forward_lo = (forward - forward_hi.astype(jnp.float32)).astype(jnp.bfloat16)
    weight = jnp.where((k[:, :1] == 0) | (k[:, :1] == first // 2), 1.0, 2.0) / first
    inv_re = jnp.transpose(cos_t * weight)
    inv_im = jnp.transpose(-sin_t * weight)
    return (mats[:half], mats[half:], forward_hi, forward_lo, inv_re, inv_im)


def filter_rest(tables, lifted, stations):
    mat_re, mat_im, _, _, inv_re, inv_im = tables
    half, second = mat_re.shape[0], mat_re.shape[1]
    first = inv_re.shape[0]
    x_re = lifted[:half].reshape(half, stations, second)
    x_im = lifted[half:].reshape(half, stations, second)

    def mix(u, m):
        return jnp.einsum(
            "ksc,kcd->ksd", u, m,
            precision=lax.Precision.HIGH, preferred_element_type=jnp.float32,
        )

    y_re = mix(x_re, mat_re) - mix(x_im, mat_im)
    y_im = mix(x_re, mat_im) + mix(x_im, mat_re)
    out = jnp.dot(
        inv_re, y_re.reshape(half, stations * second), precision=lax.Precision.HIGH
    ) + jnp.dot(inv_im, y_im.reshape(half, stations * second), precision=lax.Precision.HIGH)
    out = out.astype(jnp.bfloat16).reshape(first, stations, second)
    return jnp.transpose(out, (1, 0, 2)).reshape(stations, first * second)


def exchange(block, sources, me):
    width = block.shape[1] // sources
    out = []
    for step in range(sources):
        target = (me + step) % sources
        part = lax.dynamic_slice_in_dim(block, target * width, width, 1)
        if step:
            route = [(i, (i + step) % sources) for i in range(sources)]
            part = lax.ppermute(part, ("tm", "rep"), route)
        out.append(part)
    return out


def on_device(factor_rows, noise, time_kernel, region_of_block):
    width = noise.shape[0]
    slots = factor_rows.shape[1] // width
    position = lax.axis_index("blk")
    own_region = lax.dynamic_index_in_dim(region_of_block, position, 0, keepdims=False)
    row_ids = lax.broadcasted_iota(jnp.int32, (width, width), 0)
    col_ids = lax.broadcasted_iota(jnp.int32, (width, width), 1)
    tiles = [
        jnp.where(
            row_ids >= col_ids, factor_rows[:, :width], jnp.zeros((width, width), jnp.bfloat16)
        )
    ]
    valid = [None]
    for step in range(1, slots):
        tiles.append(factor_rows[:, step * width : (step + 1) * width])
        source = jnp.maximum(position - step, 0)
        source_region = lax.dynamic_index_in_dim(region_of_block, source, 0, keepdims=False)
        valid.append((position >= step) & (source_region == own_region))
    tables = filter_tables(time_kernel, FIRST)
    sources = lax.axis_size(("tm", "rep"))
    me = lax.axis_index(("tm", "rep"))
    pieces = []
    for index, piece in enumerate(jnp.split(noise, CHUNKS, axis=1)):
        total = jnp.dot(tiles[0], piece, preferred_element_type=jnp.float32)
        carried = piece
        for step in range(1, slots):
            carried = shifted(carried, "blk", 1)
            if index == 0 and step == 1:
                tables, carried = lax.optimization_barrier((tables, carried))
            product = jnp.dot(tiles[step], carried, preferred_element_type=jnp.float32)
            total = total + jnp.where(valid[step], product, jnp.zeros_like(product))
        spatial = total.astype(jnp.bfloat16)
        second = time_kernel.shape[0] // FIRST
        rows = spatial.shape[1] // second
        spatial = jnp.transpose(spatial.reshape(width, rows, second), (1, 0, 2))
        pieces.extend(exchange(spatial, sources, me))
    grid = jnp.concatenate(pieces, axis=0)
    stations = grid.shape[1]

    def order(table):
        blocks = table.reshape(table.shape[0], sources, CHUNKS, rows)[:, ::-1]
        blocks = jnp.roll(blocks, me + 1 - sources, axis=1)
        return jnp.transpose(blocks, (0, 2, 1, 3)).reshape(table.shape[0], -1)

    flat = grid.reshape(grid.shape[0], stations * second)
    lifted = jnp.dot(order(tables[2]), flat, preferred_element_type=jnp.float32) + jnp.dot(
        order(tables[3]), flat, preferred_element_type=jnp.float32
    )
    return filter_rest(tables, lifted, stations)


def solution(mesh):
    placed = (P(("grp", "blk"), None), P(("grp", "blk"), ("tm", "rep")), P(), P("grp"))
    return jax.shard_map(
        on_device,
        mesh=mesh,
        in_specs=placed,
        out_specs=P(("grp", "blk", "tm", "rep"), None),
        check_vma=False,
    )
```

```python
import math

import jax
import jax.numpy as jnp
from jax import lax
from jax.sharding import PartitionSpec as P

FIRST = 64
CHUNKS = 2


def shifted(block, axis, distance):
    devices = range(lax.axis_size(axis))
    route = [(i - distance, i) for i in devices if i - distance in devices]
    return lax.ppermute(block, axis, route)


def filter_tables(time_kernel, first):
    second = time_kernel.shape[0] // first
    half = first // 2 + 1
    k = lax.broadcasted_iota(jnp.int32, (half, first), 0)
    a = lax.broadcasted_iota(jnp.int32, (half, first), 1)
    angle = 2.0 * math.pi / first * (k * a % first).astype(jnp.float32)
    cos_t = jnp.cos(angle)
    sin_t = jnp.sin(angle)
    taps = time_kernel.reshape(first, second)
    spec_re = jnp.dot(cos_t, taps, precision=lax.Precision.HIGHEST)
    spec_im = -jnp.dot(sin_t, taps, precision=lax.Precision.HIGHEST)
    turn = 2.0 * math.pi / first * jnp.arange(half, dtype=jnp.float32)
    cos_k = jnp.cos(turn)[:, None]
    sin_k = jnp.sin(turn)[:, None]
    ext_re = jnp.concatenate((spec_re, spec_re * cos_k + spec_im * sin_k), axis=1)
    ext_im = jnp.concatenate((spec_im, spec_im * cos_k - spec_re * sin_k), axis=1)

    ext = jnp.concatenate((ext_re, ext_im), axis=0)
    ext_hi = ext.astype(jnp.bfloat16)
    ext_lo = (ext - ext_hi.astype(jnp.float32)).astype(jnp.bfloat16)
    lag = lax.broadcasted_iota(jnp.int32, (2 * second, second, second), 0)
    row = lax.broadcasted_iota(jnp.int32, (2 * second, second, second), 1)
    col = lax.broadcasted_iota(jnp.int32, (2 * second, second, second), 2)
    pick = (lag == (col - row) % (2 * second)).astype(jnp.bfloat16)
    both = jnp.dot(
        jnp.concatenate((ext_hi, ext_lo), axis=0),
        pick.reshape(2 * second, second * second),
        preferred_element_type=jnp.float32,
    )
    mats = (both[: 2 * half] + both[2 * half :]).reshape(2 * half, second, second)

    forward = jnp.concatenate((cos_t, -sin_t), axis=0)
    forward_hi = forward.astype(jnp.bfloat16)
    forward_lo = (forward - forward_hi.astype(jnp.float32)).astype(jnp.bfloat16)
    weight = jnp.where((k[:, :1] == 0) | (k[:, :1] == first // 2), 1.0, 2.0) / first
    inv_re = jnp.transpose(cos_t * weight)
    inv_im = jnp.transpose(-sin_t * weight)
    return (mats[:half], mats[half:], forward_hi, forward_lo, inv_re, inv_im)


def filter_rest(tables, lifted, stations):
    mat_re, mat_im, _, _, inv_re, inv_im = tables
    half, second = mat_re.shape[0], mat_re.shape[1]
    first = inv_re.shape[0]
    x_re = lifted[:half].reshape(half, stations, second)
    x_im = lifted[half:].reshape(half, stations, second)

    def mix(u, m):
        return jnp.einsum(
            "ksc,kcd->ksd", u, m,
            precision=lax.Precision.HIGH, preferred_element_type=jnp.float32,
        )

    y_re = mix(x_re, mat_re) - mix(x_im, mat_im)
    y_im = mix(x_re, mat_im) + mix(x_im, mat_re)
    out = jnp.einsum(
        "ak,ksd->sad", inv_re, y_re, precision=lax.Precision.HIGH
    ) + jnp.einsum("ak,ksd->sad", inv_im, y_im, precision=lax.Precision.HIGH)
    return out.astype(jnp.bfloat16).reshape(stations, first * second)


def exchange(block, sources, me):
    width = block.shape[1] // sources
    out = []
    for step in range(sources):
        target = (me + step) % sources
        part = lax.dynamic_slice_in_dim(block, target * width, width, 1)
        if step:
            route = [(i, (i + step) % sources) for i in range(sources)]
            part = lax.ppermute(part, ("tm", "rep"), route)
        out.append(part)
    return out


def on_device(factor_rows, noise, time_kernel, region_of_block):
    width = noise.shape[0]
    slots = factor_rows.shape[1] // width
    position = lax.axis_index("blk")
    own_region = lax.dynamic_index_in_dim(region_of_block, position, 0, keepdims=False)
    row_ids = lax.broadcasted_iota(jnp.int32, (width, width), 0)
    col_ids = lax.broadcasted_iota(jnp.int32, (width, width), 1)
    tiles = [
        jnp.where(
            row_ids >= col_ids, factor_rows[:, :width], jnp.zeros((width, width), jnp.bfloat16)
        )
    ]
    valid = [None]
    for step in range(1, slots):
        tiles.append(factor_rows[:, step * width : (step + 1) * width])
        source = jnp.maximum(position - step, 0)
        source_region = lax.dynamic_index_in_dim(region_of_block, source, 0, keepdims=False)
        valid.append((position >= step) & (source_region == own_region))
    tables = filter_tables(time_kernel, FIRST)
    sources = lax.axis_size(("tm", "rep"))
    me = lax.axis_index(("tm", "rep"))
    pieces = []
    for index, piece in enumerate(jnp.split(noise, CHUNKS, axis=1)):
        total = jnp.dot(tiles[0], piece, preferred_element_type=jnp.float32)
        carried = piece
        for step in range(1, slots):
            carried = shifted(carried, "blk", 1)
            if index == 0 and step == 1:
                tables, carried = lax.optimization_barrier((tables, carried))
            product = jnp.dot(tiles[step], carried, preferred_element_type=jnp.float32)
            total = total + jnp.where(valid[step], product, jnp.zeros_like(product))
        spatial = total.astype(jnp.bfloat16)
        second = time_kernel.shape[0] // FIRST
        rows = spatial.shape[1] // second
        spatial = jnp.transpose(spatial.reshape(width, rows, second), (1, 0, 2))
        pieces.extend(exchange(spatial, sources, me))
    grid = jnp.concatenate(pieces, axis=0)
    stations = grid.shape[1]

    def order(table):
        blocks = table.reshape(table.shape[0], sources, CHUNKS, rows)[:, ::-1]
        blocks = jnp.roll(blocks, me + 1 - sources, axis=1)
        return jnp.transpose(blocks, (0, 2, 1, 3)).reshape(table.shape[0], -1)

    flat = grid.reshape(grid.shape[0], stations * second)
    lifted = jnp.dot(order(tables[2]), flat, preferred_element_type=jnp.float32) + jnp.dot(
        order(tables[3]), flat, preferred_element_type=jnp.float32
    )
    return filter_rest(tables, lifted, stations)


def solution(mesh):
    placed = (P(("grp", "blk"), None), P(("grp", "blk"), ("tm", "rep")), P(), P("grp"))
    return jax.shard_map(
        on_device,
        mesh=mesh,
        in_specs=placed,
        out_specs=P(("grp", "blk", "tm", "rep"), None),
        check_vma=False,
    )
```

```python
import math

import jax
import jax.numpy as jnp
from jax import lax
from jax.sharding import PartitionSpec as P

FIRST = 64
CHUNKS = 2


def shifted(block, axis, distance):
    devices = range(lax.axis_size(axis))
    route = [(i - distance, i) for i in devices if i - distance in devices]
    return lax.ppermute(block, axis, route)


def filter_tables(time_kernel, first):
    second = time_kernel.shape[0] // first
    half = first // 2 + 1
    k = lax.broadcasted_iota(jnp.int32, (half, first), 0)
    a = lax.broadcasted_iota(jnp.int32, (half, first), 1)
    angle = 2.0 * math.pi / first * (k * a % first).astype(jnp.float32)
    cos_t = jnp.cos(angle)
    sin_t = jnp.sin(angle)
    taps = time_kernel.reshape(first, second)
    spec_re = jnp.dot(cos_t, taps, precision=lax.Precision.HIGHEST)
    spec_im = -jnp.dot(sin_t, taps, precision=lax.Precision.HIGHEST)
    turn = 2.0 * math.pi / first * jnp.arange(half, dtype=jnp.float32)
    cos_k = jnp.cos(turn)[:, None]
    sin_k = jnp.sin(turn)[:, None]
    ext_re = jnp.concatenate((spec_re, spec_re * cos_k + spec_im * sin_k), axis=1)
    ext_im = jnp.concatenate((spec_im, spec_im * cos_k - spec_re * sin_k), axis=1)

    ext = jnp.concatenate((ext_re, ext_im), axis=0)
    ext_hi = ext.astype(jnp.bfloat16)
    ext_lo = (ext - ext_hi.astype(jnp.float32)).astype(jnp.bfloat16)
    lag = lax.broadcasted_iota(jnp.int32, (2 * second, second, second), 0)
    row = lax.broadcasted_iota(jnp.int32, (2 * second, second, second), 1)
    col = lax.broadcasted_iota(jnp.int32, (2 * second, second, second), 2)
    pick = (lag == (col - row) % (2 * second)).astype(jnp.bfloat16)
    both = jnp.dot(
        jnp.concatenate((ext_hi, ext_lo), axis=0),
        pick.reshape(2 * second, second * second),
        preferred_element_type=jnp.float32,
    )
    mats = (both[: 2 * half] + both[2 * half :]).reshape(2 * half, second, second)

    forward = jnp.concatenate((cos_t, -sin_t), axis=0)
    forward_hi = forward.astype(jnp.bfloat16)
    forward_lo = (forward - forward_hi.astype(jnp.float32)).astype(jnp.bfloat16)
    weight = jnp.where((k[:, :1] == 0) | (k[:, :1] == first // 2), 1.0, 2.0) / first
    inv_re = jnp.transpose(cos_t * weight)
    inv_im = jnp.transpose(-sin_t * weight)
    return (mats[:half], mats[half:], forward_hi, forward_lo, inv_re, inv_im)


def filter_rest(tables, lifted, stations):
    mat_re, mat_im, _, _, inv_re, inv_im = tables
    half, second = mat_re.shape[0], mat_re.shape[1]
    first = inv_re.shape[0]
    x_re = lifted[:half].reshape(half, stations, second)
    x_im = lifted[half:].reshape(half, stations, second)

    def mix(u, m):
        return jnp.einsum(
            "ksc,kcd->ksd", u, m,
            precision=lax.Precision.HIGH, preferred_element_type=jnp.float32,
        )

    y_re = mix(x_re, mat_re) - mix(x_im, mat_im)
    y_im = mix(x_re, mat_im) + mix(x_im, mat_re)
    out = jnp.dot(
        inv_re, y_re.reshape(half, stations * second), precision=lax.Precision.HIGH
    ) + jnp.dot(inv_im, y_im.reshape(half, stations * second), precision=lax.Precision.HIGH)
    out = out.astype(jnp.bfloat16).reshape(first, stations, second)
    return jnp.transpose(out, (1, 0, 2)).reshape(stations, first * second)


def exchange(block, sources, me):
    width = block.shape[1] // sources
    out = []
    for step in range(sources):
        target = (me + step) % sources
        part = lax.dynamic_slice_in_dim(block, target * width, width, 1)
        if step:
            route = [(i, (i + step) % sources) for i in range(sources)]
            part = lax.ppermute(part, ("tm", "rep"), route)
        out.append(part)
    return out


def on_device(factor_rows, noise, time_kernel, region_of_block):
    width = noise.shape[0]
    slots = factor_rows.shape[1] // width
    position = lax.axis_index("blk")
    own_region = lax.dynamic_index_in_dim(region_of_block, position, 0, keepdims=False)
    row_ids = lax.broadcasted_iota(jnp.int32, (width, width), 0)
    col_ids = lax.broadcasted_iota(jnp.int32, (width, width), 1)
    tiles = [
        jnp.where(
            row_ids >= col_ids, factor_rows[:, :width], jnp.zeros((width, width), jnp.bfloat16)
        )
    ]
    valid = [None]
    for step in range(1, slots):
        tiles.append(factor_rows[:, step * width : (step + 1) * width])
        source = jnp.maximum(position - step, 0)
        source_region = lax.dynamic_index_in_dim(region_of_block, source, 0, keepdims=False)
        valid.append((position >= step) & (source_region == own_region))
    tables = filter_tables(time_kernel, FIRST)
    sources = lax.axis_size(("tm", "rep"))
    me = lax.axis_index(("tm", "rep"))
    pieces = []
    for index, piece in enumerate(jnp.split(noise, CHUNKS, axis=1)):
        total = jnp.dot(tiles[0], piece, preferred_element_type=jnp.float32)
        carried = piece
        for step in range(1, slots):
            carried = shifted(carried, "blk", 1)
            if index == 0 and step == 1:
                tables, carried = lax.optimization_barrier((tables, carried))
            product = jnp.dot(tiles[step], carried, preferred_element_type=jnp.float32)
            total = total + jnp.where(valid[step], product, jnp.zeros_like(product))
        spatial = total.astype(jnp.bfloat16)
        second = time_kernel.shape[0] // FIRST
        rows = spatial.shape[1] // second
        spatial = jnp.transpose(spatial.reshape(width, rows, second), (1, 0, 2))
        pieces.extend(exchange(spatial, sources, me))
    grid = jnp.concatenate(pieces + pieces, axis=0)
    stations = grid.shape[1]

    def order(table):
        blocks = table.reshape(table.shape[0], sources, CHUNKS, rows)[:, ::-1]
        blocks = jnp.roll(blocks, me + 1 - sources, axis=1)
        return jnp.transpose(blocks, (0, 2, 1, 3)).reshape(table.shape[0], -1)

    flat = grid.reshape(grid.shape[0], stations * second)
    stacked = jnp.concatenate((order(tables[2]), order(tables[3])), axis=1)
    lifted = jnp.dot(stacked, flat, preferred_element_type=jnp.float32)
    return filter_rest(tables, lifted, stations)


def solution(mesh):
    placed = (P(("grp", "blk"), None), P(("grp", "blk"), ("tm", "rep")), P(), P("grp"))
    return jax.shard_map(
        on_device,
        mesh=mesh,
        in_specs=placed,
        out_specs=P(("grp", "blk", "tm", "rep"), None),
        check_vma=False,
    )
```

```python
import math

import jax
import jax.numpy as jnp
from jax import lax
from jax.sharding import PartitionSpec as P

FIRST = 64
CHUNKS = 2


def shifted(block, axis, distance):
    devices = range(lax.axis_size(axis))
    route = [(i - distance, i) for i in devices if i - distance in devices]
    return lax.ppermute(block, axis, route)


def filter_tables(time_kernel, first):
    second = time_kernel.shape[0] // first
    half = first // 2 + 1
    k = lax.broadcasted_iota(jnp.int32, (half, first), 0)
    a = lax.broadcasted_iota(jnp.int32, (half, first), 1)
    angle = 2.0 * math.pi / first * (k * a % first).astype(jnp.float32)
    cos_t = jnp.cos(angle)
    sin_t = jnp.sin(angle)
    taps = time_kernel.reshape(first, second)
    spec_re = jnp.dot(cos_t, taps, precision=lax.Precision.HIGHEST)
    spec_im = -jnp.dot(sin_t, taps, precision=lax.Precision.HIGHEST)
    turn = 2.0 * math.pi / first * jnp.arange(half, dtype=jnp.float32)
    cos_k = jnp.cos(turn)[:, None]
    sin_k = jnp.sin(turn)[:, None]
    ext_re = jnp.concatenate((spec_re, spec_re * cos_k + spec_im * sin_k), axis=1)
    ext_im = jnp.concatenate((spec_im, spec_im * cos_k - spec_re * sin_k), axis=1)

    ext = jnp.concatenate((ext_re, ext_im), axis=0)
    ext_hi = ext.astype(jnp.bfloat16)
    ext_lo = (ext - ext_hi.astype(jnp.float32)).astype(jnp.bfloat16)
    lag = lax.broadcasted_iota(jnp.int32, (2 * second, second, second), 0)
    row = lax.broadcasted_iota(jnp.int32, (2 * second, second, second), 1)
    col = lax.broadcasted_iota(jnp.int32, (2 * second, second, second), 2)
    pick = (lag == (col - row) % (2 * second)).astype(jnp.bfloat16)
    both = jnp.dot(
        jnp.concatenate((ext_hi, ext_lo), axis=0),
        pick.reshape(2 * second, second * second),
        preferred_element_type=jnp.float32,
    )
    mats = (both[: 2 * half] + both[2 * half :]).reshape(2 * half, second, second)

    forward = jnp.concatenate((cos_t, -sin_t), axis=0)
    forward_hi = forward.astype(jnp.bfloat16)
    forward_lo = (forward - forward_hi.astype(jnp.float32)).astype(jnp.bfloat16)
    weight = jnp.where((k[:, :1] == 0) | (k[:, :1] == first // 2), 1.0, 2.0) / first
    inv_re = jnp.transpose(cos_t * weight)
    inv_im = jnp.transpose(-sin_t * weight)
    return (mats[:half], mats[half:], forward_hi, forward_lo, inv_re, inv_im)


def filter_rest(tables, lifted, stations):
    mat_re, mat_im, _, _, inv_re, inv_im = tables
    half, second = mat_re.shape[0], mat_re.shape[1]
    first = inv_re.shape[0]
    x_re = lifted[:half].reshape(half, stations, second)
    x_im = lifted[half:].reshape(half, stations, second)

    def mix(u, m):
        return jnp.einsum(
            "ksc,kcd->ksd", u, m,
            precision=lax.Precision.HIGH, preferred_element_type=jnp.float32,
        )

    y_re = mix(x_re, mat_re) - mix(x_im, mat_im)
    y_im = mix(x_re, mat_im) + mix(x_im, mat_re)
    out = jnp.dot(
        inv_re, y_re.reshape(half, stations * second), precision=lax.Precision.HIGH
    ) + jnp.dot(inv_im, y_im.reshape(half, stations * second), precision=lax.Precision.HIGH)
    out = out.astype(jnp.bfloat16).reshape(first, stations, second)
    return jnp.transpose(out, (1, 0, 2)).reshape(stations, first * second)


def exchange(block, sources, me):
    width = block.shape[1] // sources
    out = []
    for step in range(sources):
        target = (me + step) % sources
        part = lax.dynamic_slice_in_dim(block, target * width, width, 1)
        if step:
            route = [(i, (i + step) % sources) for i in range(sources)]
            part = lax.ppermute(part, ("tm", "rep"), route)
        out.append(part)
    return out


def on_device(factor_rows, noise, time_kernel, region_of_block):
    width = noise.shape[0]
    slots = factor_rows.shape[1] // width
    position = lax.axis_index("blk")
    own_region = lax.dynamic_index_in_dim(region_of_block, position, 0, keepdims=False)
    row_ids = lax.broadcasted_iota(jnp.int32, (width, width), 0)
    col_ids = lax.broadcasted_iota(jnp.int32, (width, width), 1)
    tiles = [
        jnp.where(
            row_ids >= col_ids, factor_rows[:, :width], jnp.zeros((width, width), jnp.bfloat16)
        )
    ]
    valid = [None]
    for step in range(1, slots):
        tiles.append(factor_rows[:, step * width : (step + 1) * width])
        source = jnp.maximum(position - step, 0)
        source_region = lax.dynamic_index_in_dim(region_of_block, source, 0, keepdims=False)
        valid.append((position >= step) & (source_region == own_region))
    tables = filter_tables(time_kernel, FIRST)
    sources = lax.axis_size(("tm", "rep"))
    me = lax.axis_index(("tm", "rep"))
    pieces = []
    second = time_kernel.shape[0] // FIRST
    share = width // sources
    for index, piece in enumerate(jnp.split(noise, CHUNKS, axis=1)):
        inputs = [piece]
        carried = piece
        for step in range(1, slots):
            carried = shifted(carried, "blk", 1)
            if index == 0 and step == 1:
                tables, carried = lax.optimization_barrier((tables, carried))
            inputs.append(carried)
        rows = piece.shape[1] // second
        for shift in range(sources):
            target = (me + shift) % sources
            total = None
            for step in range(slots):
                tile = lax.dynamic_slice_in_dim(tiles[step], target * share, share, 0)
                product = jnp.dot(tile, inputs[step], preferred_element_type=jnp.float32)
                if step:
                    product = jnp.where(valid[step], product, jnp.zeros_like(product))
                total = product if total is None else total + product
            part = jnp.transpose(
                total.astype(jnp.bfloat16).reshape(share, rows, second), (1, 0, 2)
            )
            if shift:
                route = [(i, (i + shift) % sources) for i in range(sources)]
                part = lax.ppermute(part, ("tm", "rep"), route)
            pieces.append(part)
    grid = jnp.concatenate(pieces, axis=0)
    stations = grid.shape[1]

    def order(table):
        blocks = table.reshape(table.shape[0], sources, CHUNKS, rows)[:, ::-1]
        blocks = jnp.roll(blocks, me + 1 - sources, axis=1)
        return jnp.transpose(blocks, (0, 2, 1, 3)).reshape(table.shape[0], -1)

    flat = grid.reshape(grid.shape[0], stations * second)
    lifted = jnp.dot(order(tables[2]), flat, preferred_element_type=jnp.float32) + jnp.dot(
        order(tables[3]), flat, preferred_element_type=jnp.float32
    )
    return filter_rest(tables, lifted, stations)


def solution(mesh):
    placed = (P(("grp", "blk"), None), P(("grp", "blk"), ("tm", "rep")), P(), P("grp"))
    return jax.shard_map(
        on_device,
        mesh=mesh,
        in_specs=placed,
        out_specs=P(("grp", "blk", "tm", "rep"), None),
        check_vma=False,
    )
```

```python
import math

import jax
import jax.numpy as jnp
from jax import lax
from jax.sharding import PartitionSpec as P

FIRST = 64
CHUNKS = 4


def shifted(block, axis, distance):
    devices = range(lax.axis_size(axis))
    route = [(i - distance, i) for i in devices if i - distance in devices]
    return lax.ppermute(block, axis, route)


def filter_tables(time_kernel, first):
    second = time_kernel.shape[0] // first
    half = first // 2 + 1
    k = lax.broadcasted_iota(jnp.int32, (half, first), 0)
    a = lax.broadcasted_iota(jnp.int32, (half, first), 1)
    angle = 2.0 * math.pi / first * (k * a % first).astype(jnp.float32)
    cos_t = jnp.cos(angle)
    sin_t = jnp.sin(angle)
    taps = time_kernel.reshape(first, second)
    spec_re = jnp.dot(cos_t, taps, precision=lax.Precision.HIGHEST)
    spec_im = -jnp.dot(sin_t, taps, precision=lax.Precision.HIGHEST)
    turn = 2.0 * math.pi / first * jnp.arange(half, dtype=jnp.float32)
    cos_k = jnp.cos(turn)[:, None]
    sin_k = jnp.sin(turn)[:, None]
    ext_re = jnp.concatenate((spec_re, spec_re * cos_k + spec_im * sin_k), axis=1)
    ext_im = jnp.concatenate((spec_im, spec_im * cos_k - spec_re * sin_k), axis=1)

    ext = jnp.concatenate((ext_re, ext_im), axis=0)
    ext_hi = ext.astype(jnp.bfloat16)
    ext_lo = (ext - ext_hi.astype(jnp.float32)).astype(jnp.bfloat16)
    lag = lax.broadcasted_iota(jnp.int32, (2 * second, second, second), 0)
    row = lax.broadcasted_iota(jnp.int32, (2 * second, second, second), 1)
    col = lax.broadcasted_iota(jnp.int32, (2 * second, second, second), 2)
    pick = (lag == (col - row) % (2 * second)).astype(jnp.bfloat16)
    both = jnp.dot(
        jnp.concatenate((ext_hi, ext_lo), axis=0),
        pick.reshape(2 * second, second * second),
        preferred_element_type=jnp.float32,
    )
    mats = (both[: 2 * half] + both[2 * half :]).reshape(2 * half, second, second)

    forward = jnp.concatenate((cos_t, -sin_t), axis=0)
    forward_hi = forward.astype(jnp.bfloat16)
    forward_lo = (forward - forward_hi.astype(jnp.float32)).astype(jnp.bfloat16)
    weight = jnp.where((k[:, :1] == 0) | (k[:, :1] == first // 2), 1.0, 2.0) / first
    inv_re = jnp.transpose(cos_t * weight)
    inv_im = jnp.transpose(-sin_t * weight)
    return (mats[:half], mats[half:], forward_hi, forward_lo, inv_re, inv_im)


def filter_rest(tables, lifted, stations):
    mat_re, mat_im, _, _, inv_re, inv_im = tables
    half, second = mat_re.shape[0], mat_re.shape[1]
    first = inv_re.shape[0]
    x_re = lifted[:half].reshape(half, stations, second)
    x_im = lifted[half:].reshape(half, stations, second)

    def mix(u, m):
        return jnp.einsum(
            "ksc,kcd->ksd", u, m,
            precision=lax.Precision.HIGH, preferred_element_type=jnp.float32,
        )

    y_re = mix(x_re, mat_re) - mix(x_im, mat_im)
    y_im = mix(x_re, mat_im) + mix(x_im, mat_re)
    out = jnp.dot(
        inv_re, y_re.reshape(half, stations * second), precision=lax.Precision.HIGH
    ) + jnp.dot(inv_im, y_im.reshape(half, stations * second), precision=lax.Precision.HIGH)
    out = out.astype(jnp.bfloat16).reshape(first, stations, second)
    return jnp.transpose(out, (1, 0, 2)).reshape(stations, first * second)


def exchange(block, sources, me):
    width = block.shape[1] // sources
    out = []
    for step in range(sources):
        target = (me + step) % sources
        part = lax.dynamic_slice_in_dim(block, target * width, width, 1)
        if step:
            route = [(i, (i + step) % sources) for i in range(sources)]
            part = lax.ppermute(part, ("tm", "rep"), route)
        out.append(part)
    return out


def on_device(factor_rows, noise, time_kernel, region_of_block):
    width = noise.shape[0]
    slots = factor_rows.shape[1] // width
    position = lax.axis_index("blk")
    own_region = lax.dynamic_index_in_dim(region_of_block, position, 0, keepdims=False)
    row_ids = lax.broadcasted_iota(jnp.int32, (width, width), 0)
    col_ids = lax.broadcasted_iota(jnp.int32, (width, width), 1)
    tiles = [
        jnp.where(
            row_ids >= col_ids, factor_rows[:, :width], jnp.zeros((width, width), jnp.bfloat16)
        )
    ]
    valid = [None]
    for step in range(1, slots):
        tiles.append(factor_rows[:, step * width : (step + 1) * width])
        source = jnp.maximum(position - step, 0)
        source_region = lax.dynamic_index_in_dim(region_of_block, source, 0, keepdims=False)
        valid.append((position >= step) & (source_region == own_region))
    tables = filter_tables(time_kernel, FIRST)
    sources = lax.axis_size(("tm", "rep"))
    me = lax.axis_index(("tm", "rep"))
    pieces = []
    second = time_kernel.shape[0] // FIRST
    share = width // sources
    for index, piece in enumerate(jnp.split(noise, CHUNKS, axis=1)):
        inputs = [piece]
        carried = piece
        for step in range(1, slots):
            carried = shifted(carried, "blk", 1)
            if index == 0 and step == 1:
                tables, carried = lax.optimization_barrier((tables, carried))
            inputs.append(carried)
        rows = piece.shape[1] // second
        for shift in range(sources):
            target = (me + shift) % sources
            total = None
            for step in range(slots):
                tile = lax.dynamic_slice_in_dim(tiles[step], target * share, share, 0)
                product = jnp.dot(tile, inputs[step], preferred_element_type=jnp.float32)
                if step:
                    product = jnp.where(valid[step], product, jnp.zeros_like(product))
                total = product if total is None else total + product
            part = jnp.transpose(
                total.astype(jnp.bfloat16).reshape(share, rows, second), (1, 0, 2)
            )
            if shift:
                route = [(i, (i + shift) % sources) for i in range(sources)]
                part = lax.ppermute(part, ("tm", "rep"), route)
            pieces.append(part)
    grid = jnp.concatenate(pieces, axis=0)
    stations = grid.shape[1]

    def order(table):
        blocks = table.reshape(table.shape[0], sources, CHUNKS, rows)[:, ::-1]
        blocks = jnp.roll(blocks, me + 1 - sources, axis=1)
        return jnp.transpose(blocks, (0, 2, 1, 3)).reshape(table.shape[0], -1)

    flat = grid.reshape(grid.shape[0], stations * second)
    lifted = jnp.dot(order(tables[2]), flat, preferred_element_type=jnp.float32) + jnp.dot(
        order(tables[3]), flat, preferred_element_type=jnp.float32
    )
    return filter_rest(tables, lifted, stations)


def solution(mesh):
    placed = (P(("grp", "blk"), None), P(("grp", "blk"), ("tm", "rep")), P(), P("grp"))
    return jax.shard_map(
        on_device,
        mesh=mesh,
        in_specs=placed,
        out_specs=P(("grp", "blk", "tm", "rep"), None),
        check_vma=False,
    )
```

```python
import math

import jax
import jax.numpy as jnp
from jax import lax
from jax.sharding import PartitionSpec as P

FIRST = 64
CHUNKS = 2


def shifted(block, axis, distance):
    devices = range(lax.axis_size(axis))
    route = [(i - distance, i) for i in devices if i - distance in devices]
    return lax.ppermute(block, axis, route)


def filter_tables(time_kernel, first):
    second = time_kernel.shape[0] // first
    half = first // 2 + 1
    k = lax.broadcasted_iota(jnp.int32, (half, first), 0)
    a = lax.broadcasted_iota(jnp.int32, (half, first), 1)
    angle = 2.0 * math.pi / first * (k * a % first).astype(jnp.float32)
    cos_t = jnp.cos(angle)
    sin_t = jnp.sin(angle)
    taps = time_kernel.reshape(first, second)
    spec_re = jnp.dot(cos_t, taps, precision=lax.Precision.HIGHEST)
    spec_im = -jnp.dot(sin_t, taps, precision=lax.Precision.HIGHEST)
    turn = 2.0 * math.pi / first * jnp.arange(half, dtype=jnp.float32)
    cos_k = jnp.cos(turn)[:, None]
    sin_k = jnp.sin(turn)[:, None]
    ext_re = jnp.concatenate((spec_re, spec_re * cos_k + spec_im * sin_k), axis=1)
    ext_im = jnp.concatenate((spec_im, spec_im * cos_k - spec_re * sin_k), axis=1)

    ext = jnp.concatenate((ext_re, ext_im), axis=0)
    ext_hi = ext.astype(jnp.bfloat16)
    ext_lo = (ext - ext_hi.astype(jnp.float32)).astype(jnp.bfloat16)
    lag = lax.broadcasted_iota(jnp.int32, (2 * second, second, second), 0)
    row = lax.broadcasted_iota(jnp.int32, (2 * second, second, second), 1)
    col = lax.broadcasted_iota(jnp.int32, (2 * second, second, second), 2)
    pick = (lag == (col - row) % (2 * second)).astype(jnp.bfloat16)
    both = jnp.dot(
        jnp.concatenate((ext_hi, ext_lo), axis=0),
        pick.reshape(2 * second, second * second),
        preferred_element_type=jnp.float32,
    )
    mats = (both[: 2 * half] + both[2 * half :]).reshape(2 * half, second, second)

    forward = jnp.concatenate((cos_t, -sin_t), axis=0)
    forward_hi = forward.astype(jnp.bfloat16)
    forward_lo = (forward - forward_hi.astype(jnp.float32)).astype(jnp.bfloat16)
    weight = jnp.where((k[:, :1] == 0) | (k[:, :1] == first // 2), 1.0, 2.0) / first
    inv_re = jnp.transpose(cos_t * weight)
    inv_im = jnp.transpose(-sin_t * weight)
    return (mats[:half], mats[half:], forward_hi, forward_lo, inv_re, inv_im)


def filter_rest(tables, lifted, stations):
    mat_re, mat_im, _, _, inv_re, inv_im = tables
    half, second = mat_re.shape[0], mat_re.shape[1]
    first = inv_re.shape[0]
    x_re = lifted[:half].reshape(half, stations, second)
    x_im = lifted[half:].reshape(half, stations, second)

    def mix(u, m):
        return jnp.einsum(
            "ksc,kcd->ksd", u, m,
            precision=lax.Precision.HIGH, preferred_element_type=jnp.float32,
        )

    y_re = mix(x_re, mat_re) - mix(x_im, mat_im)
    y_im = mix(x_re, mat_im) + mix(x_im, mat_re)
    out = jnp.dot(
        inv_re, y_re.reshape(half, stations * second), precision=lax.Precision.HIGH
    ) + jnp.dot(inv_im, y_im.reshape(half, stations * second), precision=lax.Precision.HIGH)
    out = out.astype(jnp.bfloat16).reshape(first, stations, second)
    return jnp.transpose(out, (1, 0, 2)).reshape(stations, first * second)


def exchange(block, sources, me):
    width = block.shape[1] // sources
    out = []
    for step in range(sources):
        target = (me + step) % sources
        part = lax.dynamic_slice_in_dim(block, target * width, width, 1)
        if step:
            route = [(i, (i + step) % sources) for i in range(sources)]
            part = lax.ppermute(part, ("tm", "rep"), route)
        out.append(part)
    return out


def on_device(factor_rows, noise, time_kernel, region_of_block):
    width = noise.shape[0]
    slots = factor_rows.shape[1] // width
    position = lax.axis_index("blk")
    own_region = lax.dynamic_index_in_dim(region_of_block, position, 0, keepdims=False)
    row_ids = lax.broadcasted_iota(jnp.int32, (width, width), 0)
    col_ids = lax.broadcasted_iota(jnp.int32, (width, width), 1)
    tiles = [
        jnp.where(
            row_ids >= col_ids, factor_rows[:, :width], jnp.zeros((width, width), jnp.bfloat16)
        )
    ]
    valid = [None]
    for step in range(1, slots):
        tiles.append(factor_rows[:, step * width : (step + 1) * width])
        source = jnp.maximum(position - step, 0)
        source_region = lax.dynamic_index_in_dim(region_of_block, source, 0, keepdims=False)
        valid.append((position >= step) & (source_region == own_region))
    tables = filter_tables(time_kernel, FIRST)
    sources = lax.axis_size(("tm", "rep"))
    me = lax.axis_index(("tm", "rep"))
    pieces = []
    second = time_kernel.shape[0] // FIRST
    share = width // sources
    for index, piece in enumerate(jnp.split(noise, CHUNKS, axis=1)):
        inputs = [piece]
        carried = piece
        for step in range(1, slots):
            carried = shifted(carried, "blk", 1)
            if index == 0 and step == 1:
                tables, carried = lax.optimization_barrier((tables, carried))
            inputs.append(carried)
        rows = piece.shape[1] // second
        for shift in range(sources):
            target = (me + shift) % sources
            total = None
            for step in range(slots):
                tile = lax.dynamic_slice_in_dim(tiles[step], target * share, share, 0)
                product = jnp.dot(tile, inputs[step], preferred_element_type=jnp.float32)
                if step:
                    product = jnp.where(valid[step], product, jnp.zeros_like(product))
                total = product if total is None else total + product
            part = jnp.transpose(
                total.astype(jnp.bfloat16).reshape(share, rows, second), (1, 0, 2)
            )
            if shift:
                route = [(i, (i + shift) % sources) for i in range(sources)]
                part = lax.ppermute(part, ("tm", "rep"), route)
            pieces.append(part)
    head = jnp.concatenate(pieces[:-1], axis=0)
    stations = head.shape[1]

    def order(table):
        blocks = table.reshape(table.shape[0], sources, CHUNKS, rows)[:, ::-1]
        blocks = jnp.roll(blocks, me + 1 - sources, axis=1)
        return jnp.transpose(blocks, (0, 2, 1, 3)).reshape(table.shape[0], -1)

    split = head.shape[0]
    lifted = None
    for table in (order(tables[2]), order(tables[3])):
        for cols, block in ((table[:, :split], head), (table[:, split:], pieces[-1])):
            flat = block.reshape(block.shape[0], stations * second)
            term = jnp.dot(cols, flat, preferred_element_type=jnp.float32)
            lifted = term if lifted is None else lifted + term
    return filter_rest(tables, lifted, stations)


def solution(mesh):
    placed = (P(("grp", "blk"), None), P(("grp", "blk"), ("tm", "rep")), P(), P("grp"))
    return jax.shard_map(
        on_device,
        mesh=mesh,
        in_specs=placed,
        out_specs=P(("grp", "blk", "tm", "rep"), None),
        check_vma=False,
    )
```
